256 devices in a mesh: tm: 4 (over x), tile: 64 (over y, z, core).
Axes of the slice: x: 4, y: 4, z: 8, core: 2. Of those that a mesh axis runs over, the one named last changes fastest.
Arguments:
- frame_feats: bfloat16 [4, 64, 1024, 1024], P(None, None, 'tile', 'tm'), may hold values from -6 to 6
- send_list: int32 [4, 4, 64, 3, 8], P(None, 'tm', 'tile'), may hold values from 0 to 15
- recv_slot: int32 [4, 4, 64, 16], P(None, 'tm', 'tile'), may hold values from 0 to 23, as said below
- w_unite: bfloat16 [3, 3, 64, 128], replicated, may hold values from -0.1875 to 0.1875
- w_inner: bfloat16 [3, 3, 64, 64], replicated, may hold values from -0.25 to 0.25
- w_outer: bfloat16 [3, 3, 64, 64], replicated, may hold values from -0.25 to 0.25
- w_up: bfloat16 [48, 64], replicated, may hold values from -0.75 to 0.75
Outputs:
- images: bfloat16 [4, 48, 1024, 1024], P(None, None, 'tile', 'tm')
The draws below stay inside these ranges and needn't reach their ends.
Inputs may be any that keep to these rules, and one draw needn't show every extreme that they name: `send_list`: A block index within one band's part of a strip. recv_slot = o*8 + c names entry c of list o of band j + o - 1 in the same strip; band 0 never uses o = 0 and the last band never uses o = 2; for each frame, strip and band, the entries named from one list are 0 .. k-1 with k at most 8, each named once, and some list is named in all 8 entries.
All inputs are finite; a program needn't handle non-finite values.
Results may differ from the reference program's by a relative error of at most 0.019.
Values may be sent and summed in bfloat16 or wider, within the bound.
No kernel may reach another device: no remote copies, remote signals or barrier semaphores. Data moves between devices by JAX's collectives and lax.ppermute only.
A program may use at most 64 MiB of HBM per device.

```python
import jax
import jax.numpy as jnp

C = 64
BLK = 16
NB = 16
FRAMES = 4
UP = 4
CAP = 8
HGT = 1024
WID = 1024
N_TM = 4
N_TILE = 64


def draw_recv_slot(key, part):
    key_hot = jax.random.fold_in(key, 11)
    key_split = jax.random.fold_in(key, 12)
    key_rank = jax.random.fold_in(key, 13)
    grid = (FRAMES, N_TM, N_TILE)
    hot = jax.random.randint(key_hot, grid, 0, 3)
    split = jax.random.randint(key_split, grid, 0, CAP + 1)
    first = jnp.where(hot == 0, CAP, split)
    second = jnp.where(hot == 1, CAP, jnp.where(hot == 0, split, CAP - split))
    bands = jnp.arange(N_TILE, dtype=jnp.int32)[None, None, :]
    top_band = bands == 0
    low_band = bands == N_TILE - 1
    first = jnp.where(top_band, 0, jnp.where(low_band, CAP, first))
    second = jnp.where(top_band | low_band, CAP, second)
    keys = jax.random.split(key_rank, FRAMES * N_TM * N_TILE)
    ranks = jax.vmap(lambda single: jax.random.permutation(single, NB))(keys).reshape(FRAMES, N_TM, N_TILE, NB)
    first = first[..., None]
    second = second[..., None]
    slots = jnp.where(ranks < first, ranks, jnp.where(ranks < first + second, CAP + ranks - first, 2 * CAP + ranks - first - second))
    return slots.astype(jnp.int32)


def set_ends(entries, stream_key, low, top_value):
    extent = entries.shape
    place = [jax.random.randint(jax.random.fold_in(stream_key, axis), (), 0, extent[axis]) for axis in range(len(extent))]
    entries = entries.at[tuple(place)].set(low)
    longest = extent.index(max(extent))
    place[longest] = (place[longest] + 1) % extent[longest]
    return entries.at[tuple(place)].set(top_value)


def shard_levels(own_key, shape, shards, smallest, largest):
    gain = 1.0
    for dim, blocks in shards:
        draws = jax.random.uniform(jax.random.fold_in(jax.random.fold_in(own_key, 6), dim), (blocks,), jnp.float32, smallest / len(shards), largest / len(shards))
        gain = gain * jnp.repeat(jnp.exp(draws), shape[dim] // blocks).reshape((-1,) + (1,) * (len(shape) - 1 - dim))
    return gain


def centred(own_key, shape, spread, reach, shards=(), kind=jnp.bfloat16):
    loudness = shard_levels(own_key, shape, shards, -0.22, 0.18) if shards else 1.0
    result = jax.random.normal(own_key, shape, jnp.float32) * spread * loudness
    return jnp.minimum(jnp.maximum(result, -reach), reach).astype(kind)


def setup_inputs(seed: int = 0) -> dict:
    key_of = jax.random.split(jax.random.key(seed), 8)
    frame_feats = centred(key_of[0], (FRAMES, C, HGT, WID), 1.0, 6.0, ((2, 64), (3, 4)))
    send_list = set_ends(jax.random.randint(key_of[1], (FRAMES, N_TM, N_TILE, 3, CAP), 0, NB), jax.random.fold_in(key_of[1], 1), 0, NB - 1).astype(jnp.int32)
    recv_slot = draw_recv_slot(jax.random.fold_in(key_of[7], 71), 0)
    w_unite = centred(key_of[3], (3, 3, C, 2 * C), (18 * C) ** -0.5, 0.1875)
    w_inner = centred(key_of[4], (3, 3, C, C), (9 * C) ** -0.5, 0.25)
    w_outer = centred(key_of[5], (3, 3, C, C), (9 * C) ** -0.5, 0.25)
    w_up = centred(key_of[6], (3 * UP * UP, C), C ** -0.5, 0.75)
    return {"frame_feats": frame_feats, "send_list": send_list, "recv_slot": recv_slot, "w_unite": w_unite, "w_inner": w_inner, "w_outer": w_outer, "w_up": w_up}


def convolve(source, taps):
    in_chan, rows, cols = source.shape
    padded = jnp.pad(source, ((0, 0), (1, 1), (1, 1)))
    total = jnp.zeros((taps.shape[2], rows * cols), jnp.float32)
    for row_tap in range(3):
        for col_tap in range(3):
            window = padded[:, row_tap:row_tap + rows, col_tap:col_tap + cols].reshape(in_chan, rows * cols)
            total = total + jnp.dot(taps[row_tap, col_tap], window, preferred_element_type=jnp.float32)
    return total.reshape(taps.shape[2], rows, cols)


def warp_blocks(state, lists, slots):
    blocks = state.reshape(C, N_TILE, BLK, N_TM, NB, BLK)
    strips = jnp.arange(N_TM, dtype=jnp.int32)[:, None, None]
    bands = jnp.arange(N_TILE, dtype=jnp.int32)[None, :, None]
    offset = (slots // CAP).astype(jnp.int32)
    entry = (slots % CAP).astype(jnp.int32)
    source_band = jnp.clip(bands + offset - 1, 0, N_TILE - 1).astype(jnp.int32)
    strip_full = jnp.broadcast_to(strips, offset.shape).astype(jnp.int32)
    source_block = lists[strip_full, source_band, offset, entry].astype(jnp.int32)
    picked = blocks[:, source_band, :, strip_full, source_block, :]
    return picked.transpose(3, 1, 4, 0, 2, 5).reshape(C, HGT, WID)


def reference(frame_feats, send_list, recv_slot, w_unite, w_inner, w_outer, w_up):
    state = jnp.zeros((C, HGT, WID), jnp.bfloat16)
    images = []
    for frame in range(FRAMES):
        warped = warp_blocks(state, send_list[frame], recv_slot[frame])
        joined = jnp.concatenate([warped, frame_feats[frame]], 0)
        united = convolve(joined, w_unite).astype(jnp.bfloat16)
        inner = jax.nn.relu(convolve(united, w_inner)).astype(jnp.bfloat16)
        state = (united.astype(jnp.float32) + convolve(inner, w_outer)).astype(jnp.bfloat16)
        upper = jnp.dot(w_up, state.reshape(C, HGT * WID), preferred_element_type=jnp.float32)
        images.append(upper.reshape(3 * UP * UP, HGT, WID).astype(jnp.bfloat16))
    return jnp.stack(images, 0)
```

```python
import jax
import jax.numpy as jnp
from jax import lax
from jax.sharding import PartitionSpec as P

HALO = 3


def shifted(value, moves):
    d_tm, d_tile = moves
    n_tm, n_tile = lax.axis_size("tm"), lax.axis_size("tile")
    pairs = []
    for a in range(n_tm):
        for b in range(n_tile):
            a2, b2 = a + d_tm, b + d_tile
            if 0 <= a2 < n_tm and 0 <= b2 < n_tile:
                pairs.append((a * n_tile + b, a2 * n_tile + b2))
    return lax.ppermute(value, ("tm", "tile"), pairs)


def with_halo(value, width):
    rows, cols = value.shape[-2], value.shape[-1]
    top = value[..., :width, :]
    bottom = value[..., rows - width :, :]
    left = value[..., :, :width]
    right = value[..., :, cols - width :]
    above = shifted(bottom, (0, 1))
    below = shifted(top, (0, -1))
    west = shifted(right, (1, 0))
    east = shifted(left, (-1, 0))
    nw = shifted(bottom[..., :, cols - width :], (1, 1))
    ne = shifted(bottom[..., :, :width], (-1, 1))
    sw = shifted(top[..., :, cols - width :], (1, -1))
    se = shifted(top[..., :, :width], (-1, -1))
    upper = jnp.concatenate([nw, above, ne], -1)
    middle = jnp.concatenate([west, value, east], -1)
    lower = jnp.concatenate([sw, below, se], -1)
    return jnp.concatenate([upper, middle, lower], -2)


def conv_valid(padded, taps):
    batched = padded if padded.ndim == 4 else padded[None]
    result = lax.conv_general_dilated(
        batched,
        taps,
        (1, 1),
        "VALID",
        dimension_numbers=("NCHW", "HWOI", "NCHW"),
        preferred_element_type=jnp.float32,
    )
    return result if padded.ndim == 4 else result[0]


def inside_crop(rows, cols, margin):
    n_tm, n_tile = lax.axis_size("tm"), lax.axis_size("tile")
    band, strip = lax.axis_index("tile"), lax.axis_index("tm")
    r = band * rows - margin + jnp.arange(rows + 2 * margin, dtype=jnp.int32)
    c = strip * cols - margin + jnp.arange(cols + 2 * margin, dtype=jnp.int32)
    ok_r = (r >= 0) & (r < rows * n_tile)
    ok_c = (c >= 0) & (c < cols * n_tm)
    return ok_r[:, None] & ok_c[None, :]


def from_behind(value, axis, by):
    size = lax.axis_size(axis)
    pairs = [(i, i + by) for i in range(size) if 0 <= i + by < size]
    return lax.ppermute(value, axis, pairs)


def move_blocks(state, lists, slots):
    chan, rows, cols = state.shape
    entries = lists.shape[1]
    width = entries * rows
    flat = state.reshape(chan * rows, cols)
    inside = jnp.arange(rows, dtype=jnp.int32)
    targets = (lists.reshape(-1)[:, None] * rows + inside[None, :]).reshape(-1)
    columns = jnp.arange(cols, dtype=jnp.int32)
    picker = (columns[:, None] == targets[None, :]).astype(jnp.bfloat16)
    offered = jnp.dot(flat, picker, preferred_element_type=jnp.float32).astype(jnp.bfloat16)
    outgoing = [offered[:, offset * width : (offset + 1) * width] for offset in range(3)]
    pieces = []
    for offset in range(3):
        if offset == 1:
            pieces.append(outgoing[1])
        else:
            pieces.append(from_behind(outgoing[offset], "tile", 1 - offset))
    pool = jnp.concatenate(pieces, 1)
    sources = slots[columns // rows] * rows + columns % rows
    pool_index = jnp.arange(3 * width, dtype=jnp.int32)
    placer = (pool_index[:, None] == sources[None, :]).astype(jnp.bfloat16)
    warped = jnp.dot(pool, placer, preferred_element_type=jnp.float32).astype(jnp.bfloat16)
    return warped.reshape(chan, rows, cols)


def on_device(frame_feats, send_list, recv_slot, w_unite, w_inner, w_outer, w_up):
    frames, chan, rows, cols = frame_feats.shape
    h = HALO
    w_warp = w_unite[:, :, :, :chan]
    w_feat = w_unite[:, :, :, chan:]
    feats_ext = with_halo(frame_feats, h)
    feat_part = conv_valid(feats_ext, w_feat)
    mask1 = inside_crop(rows, cols, h - 1)
    mask2 = inside_crop(rows, cols, h - 2)
    images = []
    state = None
    for t in range(frames):
        united_f = feat_part[t]
        if t > 0:
            warped = move_blocks(state, send_list[t, 0, 0], recv_slot[t, 0, 0])
            warped_ext = with_halo(warped, h)
            united_f = united_f + conv_valid(warped_ext, w_warp)
        united = jnp.where(mask1, united_f, 0.0).astype(jnp.bfloat16)
        inner_f = jnp.maximum(conv_valid(united, w_inner), 0.0)
        inner = jnp.where(mask2, inner_f, 0.0).astype(jnp.bfloat16)
        core = united[:, 2 : 2 + rows, 2 : 2 + cols].astype(jnp.float32)
        state = (core + conv_valid(inner, w_outer)).astype(jnp.bfloat16)
        upper = jnp.dot(w_up, state.reshape(chan, rows * cols), preferred_element_type=jnp.float32)
        images.append(upper.reshape(w_up.shape[0], rows, cols).astype(jnp.bfloat16))
    return jnp.stack(images, 0)


def solution(mesh):
    placed = (
        P(None, None, "tile", "tm"),
        P(None, "tm", "tile", None, None),
        P(None, "tm", "tile", None),
        P(),
        P(),
        P(),
        P(),
    )
    return jax.shard_map(
        on_device,
        mesh=mesh,
        in_specs=placed,
        out_specs=P(None, None, "tile", "tm"),
        check_vma=False,
    )
```

```python
import jax
import jax.numpy as jnp
from jax import lax
from jax.sharding import PartitionSpec as P

HALO = 3


def shifted(value, moves):
    d_tm, d_tile = moves
    n_tm, n_tile = lax.axis_size("tm"), lax.axis_size("tile")
    pairs = []
    for a in range(n_tm):
        for b in range(n_tile):
            a2, b2 = a + d_tm, b + d_tile
            if 0 <= a2 < n_tm and 0 <= b2 < n_tile:
                pairs.append((a * n_tile + b, a2 * n_tile + b2))
    return lax.ppermute(value, ("tm", "tile"), pairs)


def with_halo(value, width):
    rows, cols = value.shape[-2], value.shape[-1]
    top = value[..., :width, :]
    bottom = value[..., rows - width :, :]
    left = value[..., :, :width]
    right = value[..., :, cols - width :]
    above = shifted(bottom, (0, 1))
    below = shifted(top, (0, -1))
    west = shifted(right, (1, 0))
    east = shifted(left, (-1, 0))
    nw = shifted(bottom[..., :, cols - width :], (1, 1))
    ne = shifted(bottom[..., :, :width], (-1, 1))
    sw = shifted(top[..., :, cols - width :], (1, -1))
    se = shifted(top[..., :, :width], (-1, -1))
    upper = jnp.concatenate([nw, above, ne], -1)
    middle = jnp.concatenate([west, value, east], -1)
    lower = jnp.concatenate([sw, below, se], -1)
    return jnp.concatenate([upper, middle, lower], -2)


def conv_valid(padded, taps):
    batched = padded if padded.ndim == 4 else padded[None]
    result = lax.conv_general_dilated(
        batched,
        taps,
        (1, 1),
        "VALID",
        dimension_numbers=("NCHW", "HWOI", "NCHW"),
        preferred_element_type=jnp.float32,
    )
    return result if padded.ndim == 4 else result[0]


def inside_crop(rows, cols, margin):
    n_tm, n_tile = lax.axis_size("tm"), lax.axis_size("tile")
    band, strip = lax.axis_index("tile"), lax.axis_index("tm")
    r = band * rows - margin + jnp.arange(rows + 2 * margin, dtype=jnp.int32)
    c = strip * cols - margin + jnp.arange(cols + 2 * margin, dtype=jnp.int32)
    ok_r = (r >= 0) & (r < rows * n_tile)
    ok_c = (c >= 0) & (c < cols * n_tm)
    return ok_r[:, None] & ok_c[None, :]


def from_behind(value, axis, by):
    size = lax.axis_size(axis)
    pairs = [(i, i + by) for i in range(size) if 0 <= i + by < size]
    return lax.ppermute(value, axis, pairs)


def move_blocks(state, lists, slots):
    chan, rows, cols = state.shape
    entries = lists.shape[1]
    width = entries * rows
    flat = state.reshape(chan * rows, cols)
    inside = jnp.arange(rows, dtype=jnp.int32)
    targets = (lists.reshape(-1)[:, None] * rows + inside[None, :]).reshape(-1)
    columns = jnp.arange(cols, dtype=jnp.int32)
    picker = (columns[:, None] == targets[None, :]).astype(jnp.bfloat16)
    offered = jnp.dot(flat, picker, preferred_element_type=jnp.float32).astype(jnp.bfloat16)
    outgoing = [offered[:, offset * width : (offset + 1) * width] for offset in range(3)]
    pieces = []
    for offset in range(3):
        if offset == 1:
            pieces.append(outgoing[1])
        else:
            pieces.append(from_behind(outgoing[offset], "tile", 1 - offset))
    pool = jnp.concatenate(pieces, 1)
    sources = slots[columns // rows] * rows + columns % rows
    pool_index = jnp.arange(3 * width, dtype=jnp.int32)
    placer = (pool_index[:, None] == sources[None, :]).astype(jnp.bfloat16)
    warped = jnp.dot(pool, placer, preferred_element_type=jnp.float32).astype(jnp.bfloat16)
    return warped.reshape(chan, rows, cols)


def on_device(frame_feats, send_list, recv_slot, w_unite, w_inner, w_outer, w_up):
    frames, chan, rows, cols = frame_feats.shape
    h = HALO
    mask1 = inside_crop(rows, cols, h - 1)
    mask2 = inside_crop(rows, cols, h - 2)

    def finish(united_f):
        united = jnp.where(mask1, united_f, 0.0).astype(jnp.bfloat16)
        inner_f = jnp.maximum(conv_valid(united, w_inner), 0.0)
        inner = jnp.where(mask2, inner_f, 0.0).astype(jnp.bfloat16)
        core = united[:, 2 : 2 + rows, 2 : 2 + cols].astype(jnp.float32)
        state = (core + conv_valid(inner, w_outer)).astype(jnp.bfloat16)
        upper = jnp.dot(w_up, state.reshape(chan, rows * cols), preferred_element_type=jnp.float32)
        return state, upper.reshape(w_up.shape[0], rows, cols).astype(jnp.bfloat16)

    feats_ext = with_halo(frame_feats[0], h)
    state, first = finish(conv_valid(feats_ext, w_unite[:, :, :, chan:]))

    def advance(state, inputs):
        feats, lists, slots = inputs
        warped = move_blocks(state, lists, slots)
        joined_ext = with_halo(jnp.concatenate([warped, feats], 0), h)
        return finish(conv_valid(joined_ext, w_unite))

    _, rest = lax.scan(
        advance, state, (frame_feats[1:], send_list[1:, 0, 0], recv_slot[1:, 0, 0])
    )
    return jnp.concatenate([first[None], rest], 0)


def solution(mesh):
    placed = (
        P(None, None, "tile", "tm"),
        P(None, "tm", "tile", None, None),
        P(None, "tm", "tile", None),
        P(),
        P(),
        P(),
        P(),
    )
    return jax.shard_map(
        on_device,
        mesh=mesh,
        in_specs=placed,
        out_specs=P(None, None, "tile", "tm"),
        check_vma=False,
    )
```

```python
import jax
import jax.numpy as jnp
from jax import lax
from jax.sharding import PartitionSpec as P

HALO = 3


def shifted(value, moves):
    d_tm, d_tile = moves
    n_tm, n_tile = lax.axis_size("tm"), lax.axis_size("tile")
    pairs = []
    for a in range(n_tm):
        for b in range(n_tile):
            a2, b2 = a + d_tm, b + d_tile
            if 0 <= a2 < n_tm and 0 <= b2 < n_tile:
                pairs.append((a * n_tile + b, a2 * n_tile + b2))
    return lax.ppermute(value, ("tm", "tile"), pairs)


def with_halo(value, width):
    rows, cols = value.shape[-2], value.shape[-1]
    top = value[..., :width, :]
    bottom = value[..., rows - width :, :]
    left = value[..., :, :width]
    right = value[..., :, cols - width :]
    above = shifted(bottom, (0, 1))
    below = shifted(top, (0, -1))
    west = shifted(right, (1, 0))
    east = shifted(left, (-1, 0))
    nw = shifted(bottom[..., :, cols - width :], (1, 1))
    ne = shifted(bottom[..., :, :width], (-1, 1))
    sw = shifted(top[..., :, cols - width :], (1, -1))
    se = shifted(top[..., :, :width], (-1, -1))
    upper = jnp.concatenate([nw, above, ne], -1)
    middle = jnp.concatenate([west, value, east], -1)
    lower = jnp.concatenate([sw, below, se], -1)
    return jnp.concatenate([upper, middle, lower], -2)


def conv_valid(padded, taps):
    batched = padded if padded.ndim == 4 else padded[None]
    result = lax.conv_general_dilated(
        batched,
        taps,
        (1, 1),
        "VALID",
        dimension_numbers=("NCHW", "HWOI", "NCHW"),
        preferred_element_type=jnp.float32,
    )
    return result if padded.ndim == 4 else result[0]


def inside_crop(rows, cols, margin):
    n_tm, n_tile = lax.axis_size("tm"), lax.axis_size("tile")
    band, strip = lax.axis_index("tile"), lax.axis_index("tm")
    r = band * rows - margin + jnp.arange(rows + 2 * margin, dtype=jnp.int32)
    c = strip * cols - margin + jnp.arange(cols + 2 * margin, dtype=jnp.int32)
    ok_r = (r >= 0) & (r < rows * n_tile)
    ok_c = (c >= 0) & (c < cols * n_tm)
    return ok_r[:, None] & ok_c[None, :]


def from_behind(value, axis, by):
    size = lax.axis_size(axis)
    pairs = [(i, i + by) for i in range(size) if 0 <= i + by < size]
    return lax.ppermute(value, axis, pairs)


def block_onehot(rows_of, cols_of, blk):
    pick = rows_of[:, None] == cols_of[None, :]
    eye = jnp.arange(blk)[:, None] == jnp.arange(blk)[None, :]
    full = pick[:, None, :, None] & eye[None, :, None, :]
    return full.reshape(rows_of.shape[0] * blk, cols_of.shape[0] * blk).astype(jnp.bfloat16)


def move_blocks(state, lists, slots):
    chan, rows, cols = state.shape
    entries = lists.shape[1]
    width = entries * rows
    blocks = cols // rows
    flat = state.reshape(chan * rows, cols)
    picker = block_onehot(jnp.arange(blocks, dtype=jnp.int32), lists.reshape(-1), rows)
    offered = jnp.dot(flat, picker, preferred_element_type=jnp.float32).astype(jnp.bfloat16)
    outgoing = [offered[:, offset * width : (offset + 1) * width] for offset in range(3)]
    pieces = []
    for offset in range(3):
        if offset == 1:
            pieces.append(outgoing[1])
        else:
            pieces.append(from_behind(outgoing[offset], "tile", 1 - offset))
    pool = jnp.concatenate(pieces, 1)
    placer = block_onehot(jnp.arange(3 * entries, dtype=jnp.int32), slots, rows)
    warped = jnp.dot(pool, placer, preferred_element_type=jnp.float32).astype(jnp.bfloat16)
    return warped.reshape(chan, rows, cols)


def on_device(frame_feats, send_list, recv_slot, w_unite, w_inner, w_outer, w_up):
    frames, chan, rows, cols = frame_feats.shape
    h = HALO
    mask1 = inside_crop(rows, cols, h - 1)
    mask2 = inside_crop(rows, cols, h - 2)

    def finish(united_f):
        united = jnp.where(mask1, united_f, 0.0).astype(jnp.bfloat16)
        inner_f = jnp.maximum(conv_valid(united, w_inner), 0.0)
        inner = jnp.where(mask2, inner_f, 0.0).astype(jnp.bfloat16)
        core = united[:, 2 : 2 + rows, 2 : 2 + cols].astype(jnp.float32)
        state = (core + conv_valid(inner, w_outer)).astype(jnp.bfloat16)
        upper = jnp.dot(w_up, state.reshape(chan, rows * cols), preferred_element_type=jnp.float32)
        return state, upper.reshape(w_up.shape[0], rows, cols).astype(jnp.bfloat16)

    feats_ext = with_halo(frame_feats[0], h)
    state, first = finish(conv_valid(feats_ext, w_unite[:, :, :, chan:]))

    def advance(state, inputs):
        feats, lists, slots = inputs
        warped = move_blocks(state, lists, slots)
        joined_ext = with_halo(jnp.concatenate([warped, feats], 0), h)
        return finish(conv_valid(joined_ext, w_unite))

    _, rest = lax.scan(
        advance, state, (frame_feats[1:], send_list[1:, 0, 0], recv_slot[1:, 0, 0])
    )
    return jnp.concatenate([first[None], rest], 0)


def solution(mesh):
    placed = (
        P(None, None, "tile", "tm"),
        P(None, "tm", "tile", None, None),
        P(None, "tm", "tile", None),
        P(),
        P(),
        P(),
        P(),
    )
    return jax.shard_map(
        on_device,
        mesh=mesh,
        in_specs=placed,
        out_specs=P(None, None, "tile", "tm"),
        check_vma=False,
    )
```

```python
import jax
import jax.numpy as jnp
from jax import lax
from jax.sharding import PartitionSpec as P

HALO = 3


def shifted(value, moves):
    d_tm, d_tile = moves
    n_tm, n_tile = lax.axis_size("tm"), lax.axis_size("tile")
    pairs = []
    for a in range(n_tm):
        for b in range(n_tile):
            a2, b2 = a + d_tm, b + d_tile
            if 0 <= a2 < n_tm and 0 <= b2 < n_tile:
                pairs.append((a * n_tile + b, a2 * n_tile + b2))
    return lax.ppermute(value, ("tm", "tile"), pairs)


def with_halo(value, width):
    cols = value.shape[-1]
    west = shifted(value[..., :, cols - width :], (1, 0))
    east = shifted(value[..., :, :width], (-1, 0))
    middle = jnp.concatenate([west, value, east], -1)
    rows = middle.shape[-2]
    above = shifted(middle[..., rows - width :, :], (0, 1))
    below = shifted(middle[..., :width, :], (0, -1))
    return jnp.concatenate([above, middle, below], -2)


def conv_valid(padded, taps):
    batched = padded if padded.ndim == 4 else padded[None]
    result = lax.conv_general_dilated(
        batched,
        taps,
        (1, 1),
        "VALID",
        dimension_numbers=("NCHW", "HWOI", "NCHW"),
        preferred_element_type=jnp.float32,
    )
    return result if padded.ndim == 4 else result[0]


def inside_crop(rows, cols, margin):
    n_tm, n_tile = lax.axis_size("tm"), lax.axis_size("tile")
    band, strip = lax.axis_index("tile"), lax.axis_index("tm")
    r = band * rows - margin + jnp.arange(rows + 2 * margin, dtype=jnp.int32)
    c = strip * cols - margin + jnp.arange(cols + 2 * margin, dtype=jnp.int32)
    ok_r = (r >= 0) & (r < rows * n_tile)
    ok_c = (c >= 0) & (c < cols * n_tm)
    return ok_r[:, None] & ok_c[None, :]


def from_behind(value, axis, by):
    size = lax.axis_size(axis)
    pairs = [(i, i + by) for i in range(size) if 0 <= i + by < size]
    return lax.ppermute(value, axis, pairs)


def block_onehot(rows_of, cols_of, blk):
    pick = rows_of[:, None] == cols_of[None, :]
    eye = jnp.arange(blk)[:, None] == jnp.arange(blk)[None, :]
    full = pick[:, None, :, None] & eye[None, :, None, :]
    return full.reshape(rows_of.shape[0] * blk, cols_of.shape[0] * blk).astype(jnp.bfloat16)


def move_blocks(state, lists, slots):
    chan, rows, cols = state.shape
    entries = lists.shape[1]
    width = entries * rows
    blocks = cols // rows
    flat = state.reshape(chan * rows, cols)
    picker = block_onehot(jnp.arange(blocks, dtype=jnp.int32), lists.reshape(-1), rows)
    offered = jnp.dot(flat, picker, preferred_element_type=jnp.float32).astype(jnp.bfloat16)
    outgoing = [offered[:, offset * width : (offset + 1) * width] for offset in range(3)]
    pieces = []
    for offset in range(3):
        if offset == 1:
            pieces.append(outgoing[1])
        else:
            pieces.append(from_behind(outgoing[offset], "tile", 1 - offset))
    pool = jnp.concatenate(pieces, 1)
    placer = block_onehot(jnp.arange(3 * entries, dtype=jnp.int32), slots, rows)
    warped = jnp.dot(pool, placer, preferred_element_type=jnp.float32).astype(jnp.bfloat16)
    return warped.reshape(chan, rows, cols)


def on_device(frame_feats, send_list, recv_slot, w_unite, w_inner, w_outer, w_up):
    frames, chan, rows, cols = frame_feats.shape
    h = HALO
    mask1 = inside_crop(rows, cols, h - 1)
    mask2 = inside_crop(rows, cols, h - 2)

    def finish(united_f):
        united = jnp.where(mask1, united_f, 0.0).astype(jnp.bfloat16)
        inner_f = jnp.maximum(conv_valid(united, w_inner), 0.0)
        inner = jnp.where(mask2, inner_f, 0.0).astype(jnp.bfloat16)
        core = united[:, 2 : 2 + rows, 2 : 2 + cols].astype(jnp.float32)
        state = (core + conv_valid(inner, w_outer)).astype(jnp.bfloat16)
        upper = jnp.dot(w_up, state.reshape(chan, rows * cols), preferred_element_type=jnp.float32)
        return state, upper.reshape(w_up.shape[0], rows, cols).astype(jnp.bfloat16)

    feats_ext = with_halo(frame_feats[0], h)
    state, first = finish(conv_valid(feats_ext, w_unite[:, :, :, chan:]))

    def advance(state, inputs):
        feats, lists, slots = inputs
        warped = move_blocks(state, lists, slots)
        joined_ext = with_halo(jnp.concatenate([warped, feats], 0), h)
        return finish(conv_valid(joined_ext, w_unite))

    _, rest = lax.scan(
        advance, state, (frame_feats[1:], send_list[1:, 0, 0], recv_slot[1:, 0, 0])
    )
    return jnp.concatenate([first[None], rest], 0)


def solution(mesh):
    placed = (
        P(None, None, "tile", "tm"),
        P(None, "tm", "tile", None, None),
        P(None, "tm", "tile", None),
        P(),
        P(),
        P(),
        P(),
    )
    return jax.shard_map(
        on_device,
        mesh=mesh,
        in_specs=placed,
        out_specs=P(None, None, "tile", "tm"),
        check_vma=False,
    )
```

```python
import jax
import jax.numpy as jnp
from jax import lax
from jax.sharding import PartitionSpec as P

HALO = 3


def shifted(value, moves):
    d_tm, d_tile = moves
    n_tm, n_tile = lax.axis_size("tm"), lax.axis_size("tile")
    pairs = []
    for a in range(n_tm):
        for b in range(n_tile):
            a2, b2 = a + d_tm, b + d_tile
            if 0 <= a2 < n_tm and 0 <= b2 < n_tile:
                pairs.append((a * n_tile + b, a2 * n_tile + b2))
    return lax.ppermute(value, ("tm", "tile"), pairs)


def with_halo(value, width):
    cols = value.shape[-1]
    west = shifted(value[..., :, cols - width :], (1, 0))
    east = shifted(value[..., :, :width], (-1, 0))
    middle = jnp.concatenate([west, value, east], -1)
    rows = middle.shape[-2]
    above = shifted(middle[..., rows - width :, :], (0, 1))
    below = shifted(middle[..., :width, :], (0, -1))
    return jnp.concatenate([above, middle, below], -2)


def conv_valid(padded, taps):
    batched = padded if padded.ndim == 4 else padded[None]
    result = lax.conv_general_dilated(
        batched,
        taps,
        (1, 1),
        "VALID",
        dimension_numbers=("NCHW", "HWOI", "NCHW"),
        preferred_element_type=jnp.float32,
    )
    return result if padded.ndim == 4 else result[0]


def inside_crop(rows, cols, margin):
    n_tm, n_tile = lax.axis_size("tm"), lax.axis_size("tile")
    band, strip = lax.axis_index("tile"), lax.axis_index("tm")
    r = band * rows - margin + jnp.arange(rows + 2 * margin, dtype=jnp.int32)
    c = strip * cols - margin + jnp.arange(cols + 2 * margin, dtype=jnp.int32)
    ok_r = (r >= 0) & (r < rows * n_tile)
    ok_c = (c >= 0) & (c < cols * n_tm)
    return ok_r[:, None] & ok_c[None, :]


def from_behind(value, axis, by):
    size = lax.axis_size(axis)
    pairs = [(i, i + by) for i in range(size) if 0 <= i + by < size]
    return lax.ppermute(value, axis, pairs)


def block_onehot(rows_of, cols_of, blk):
    pick = rows_of[..., :, None] == cols_of[..., None, :]
    eye = jnp.arange(blk)[:, None] == jnp.arange(blk)[None, :]
    full = pick[..., :, None, :, None] & eye[:, None, :]
    lead = full.shape[:-4]
    return full.reshape(lead + (pick.shape[-2] * blk, pick.shape[-1] * blk)).astype(jnp.bfloat16)


def move_onehots(lists, slots, rows, blocks):
    frames = lists.shape[0]
    picker = block_onehot(jnp.arange(blocks, dtype=jnp.int32), lists.reshape(frames, -1), rows)
    pool_ids = jnp.arange(lists.shape[1] * lists.shape[2], dtype=jnp.int32)
    placer = block_onehot(pool_ids, slots, rows)
    return picker, placer


def move_blocks(state, picker, placer, entries):
    chan, rows, cols = state.shape
    width = entries * rows
    flat = state.reshape(chan * rows, cols)
    offered = jnp.dot(flat, picker, preferred_element_type=jnp.float32).astype(jnp.bfloat16)
    outgoing = [offered[:, offset * width : (offset + 1) * width] for offset in range(3)]
    pieces = []
    for offset in range(3):
        if offset == 1:
            pieces.append(outgoing[1])
        else:
            pieces.append(from_behind(outgoing[offset], "tile", 1 - offset))
    pool = jnp.concatenate(pieces, 1)
    warped = jnp.dot(pool, placer, preferred_element_type=jnp.float32).astype(jnp.bfloat16)
    return warped.reshape(chan, rows, cols)


def on_device(frame_feats, send_list, recv_slot, w_unite, w_inner, w_outer, w_up):
    frames, chan, rows, cols = frame_feats.shape
    h = HALO
    mask1 = inside_crop(rows, cols, h - 1)
    mask2 = inside_crop(rows, cols, h - 2)

    def finish(united_f):
        united = jnp.where(mask1, united_f, 0.0).astype(jnp.bfloat16)
        inner_f = jnp.maximum(conv_valid(united, w_inner), 0.0)
        inner = jnp.where(mask2, inner_f, 0.0).astype(jnp.bfloat16)
        core = united[:, 2 : 2 + rows, 2 : 2 + cols].astype(jnp.float32)
        state = (core + conv_valid(inner, w_outer)).astype(jnp.bfloat16)
        upper = jnp.dot(w_up, state.reshape(chan, rows * cols), preferred_element_type=jnp.float32)
        return state, upper.reshape(w_up.shape[0], rows, cols).astype(jnp.bfloat16)

    feats_ext = with_halo(frame_feats[0], h)
    state, first = finish(conv_valid(feats_ext, w_unite[:, :, :, chan:]))

    entries = send_list.shape[-1]
    pickers, placers = move_onehots(send_list[1:, 0, 0], recv_slot[1:, 0, 0], rows, cols // rows)

    def advance(state, inputs):
        feats, picker, placer = inputs
        warped = move_blocks(state, picker, placer, entries)
        joined_ext = with_halo(jnp.concatenate([warped, feats], 0), h)
        return finish(conv_valid(joined_ext, w_unite))

    _, rest = lax.scan(
        advance, state, (frame_feats[1:], pickers, placers)
    )
    return jnp.concatenate([first[None], rest], 0)


def solution(mesh):
    placed = (
        P(None, None, "tile", "tm"),
        P(None, "tm", "tile", None, None),
        P(None, "tm", "tile", None),
        P(),
        P(),
        P(),
        P(),
    )
    return jax.shard_map(
        on_device,
        mesh=mesh,
        in_specs=placed,
        out_specs=P(None, None, "tile", "tm"),
        check_vma=False,
    )
```

```python
import jax
import jax.numpy as jnp
from jax import lax
from jax.sharding import PartitionSpec as P
from jax.experimental import pallas as pl
from jax.experimental.pallas import tpu as pltpu

HALO = 3


def shifted(value, moves):
    d_tm, d_tile = moves
    n_tm, n_tile = lax.axis_size("tm"), lax.axis_size("tile")
    pairs = []
    for a in range(n_tm):
        for b in range(n_tile):
            a2, b2 = a + d_tm, b + d_tile
            if 0 <= a2 < n_tm and 0 <= b2 < n_tile:
                pairs.append((a * n_tile + b, a2 * n_tile + b2))
    return lax.ppermute(value, ("tm", "tile"), pairs)


def with_halo(value, width):
    cols = value.shape[-1]
    west = shifted(value[..., cols - width :], (1, 0))
    east = shifted(value[..., :width], (-1, 0))
    middle = jnp.concatenate([west, value, east], -1)
    rows = middle.shape[0]
    above = shifted(middle[rows - width :], (0, 1))
    below = shifted(middle[:width], (0, -1))
    return jnp.concatenate([above, middle, below], 0)


LANES = 384


def tap_row(src_ref, w_ref, y):
    acc = None
    for a in range(3):
        row = src_ref[y + a]
        for b in range(3):
            part = jnp.dot(w_ref[a * 3 + b], row, preferred_element_type=jnp.float32)
            if b:
                part = pltpu.roll(part, LANES - b, 1)
            acc = part if acc is None else acc + part
    return acc


def chain_kernel(x_ref, m1_ref, m2_ref, w1_ref, w2_ref, w3_ref, wup_ref, state_ref, img_ref, u_ref, i_ref):
    def conv1(y, carry):
        u_ref[y] = (tap_row(x_ref, w1_ref, y) * m1_ref[y]).astype(jnp.bfloat16)
        return carry

    def conv2(y, carry):
        i_ref[y] = (jnp.maximum(tap_row(u_ref, w2_ref, y), 0.0) * m2_ref[y]).astype(jnp.bfloat16)
        return carry

    def conv3(y, carry):
        res = pltpu.roll(u_ref[y + 2].astype(jnp.float32), LANES - 2, 1)
        st = (res + tap_row(i_ref, w3_ref, y)).astype(jnp.bfloat16)
        state_ref[y] = st
        img_ref[y] = jnp.dot(wup_ref[...], st, preferred_element_type=jnp.float32).astype(jnp.bfloat16)
        return carry

    lax.fori_loop(0, u_ref.shape[0], conv1, 0)
    lax.fori_loop(0, i_ref.shape[0], conv2, 0)
    lax.fori_loop(0, state_ref.shape[0], conv3, 0)


def conv_chain(x_ext, m1, m2, w1, w2, w3, wup):
    rows = x_ext.shape[0] - 6
    chan, planes = w2.shape[1], wup.shape[0]
    return pl.pallas_call(
        chain_kernel,
        out_shape=(
            jax.ShapeDtypeStruct((rows, chan, LANES), jnp.bfloat16),
            jax.ShapeDtypeStruct((rows, planes, LANES), jnp.bfloat16),
        ),
        scratch_shapes=[
            pltpu.VMEM((rows + 4, chan, LANES), jnp.bfloat16),
            pltpu.VMEM((rows + 2, chan, LANES), jnp.bfloat16),
        ],
    )(x_ext, m1, m2, w1, w2, w3, wup)


def conv_valid(padded, taps):
    batched = padded if padded.ndim == 4 else padded[None]
    result = lax.conv_general_dilated(
        batched,
        taps,
        (1, 1),
        "VALID",
        dimension_numbers=("NCHW", "HWOI", "NCHW"),
        preferred_element_type=jnp.float32,
    )
    return result if padded.ndim == 4 else result[0]


def inside_crop(rows, cols, margin):
    n_tm, n_tile = lax.axis_size("tm"), lax.axis_size("tile")
    band, strip = lax.axis_index("tile"), lax.axis_index("tm")
    r = band * rows - margin + jnp.arange(rows + 2 * margin, dtype=jnp.int32)
    x = jnp.arange(LANES, dtype=jnp.int32)
    c = strip * cols - margin + x
    ok_r = (r >= 0) & (r < rows * n_tile)
    ok_c = (c >= 0) & (c < cols * n_tm) & (x < cols + 2 * margin)
    return (ok_r[:, None] & ok_c[None, :]).astype(jnp.float32)[:, None, :]


def from_behind(value, axis, by):
    size = lax.axis_size(axis)
    pairs = [(i, i + by) for i in range(size) if 0 <= i + by < size]
    return lax.ppermute(value, axis, pairs)


def block_onehot(rows_of, cols_of, blk):
    pick = rows_of[:, None] == cols_of[None, :]
    eye = jnp.arange(blk)[:, None] == jnp.arange(blk)[None, :]
    full = pick[:, None, :, None] & eye[None, :, None, :]
    return full.reshape(rows_of.shape[0] * blk, cols_of.shape[0] * blk).astype(jnp.bfloat16)


def move_blocks(state, lists, slots):
    rows, chan, cols = state.shape
    entries = lists.shape[1]
    width = entries * rows
    blocks = cols // rows
    flat = state.reshape(rows * chan, cols)
    picker = block_onehot(jnp.arange(blocks, dtype=jnp.int32), lists.reshape(-1), rows)
    offered = jnp.dot(flat, picker, preferred_element_type=jnp.float32).astype(jnp.bfloat16)
    outgoing = [offered[:, offset * width : (offset + 1) * width] for offset in range(3)]
    pieces = []
    for offset in range(3):
        if offset == 1:
            pieces.append(outgoing[1])
        else:
            pieces.append(from_behind(outgoing[offset], "tile", 1 - offset))
    pool = jnp.concatenate(pieces, 1)
    placer = block_onehot(jnp.arange(3 * entries, dtype=jnp.int32), slots, rows)
    warped = jnp.dot(pool, placer, preferred_element_type=jnp.float32).astype(jnp.bfloat16)
    return warped.reshape(state.shape)


def on_device(frame_feats, send_list, recv_slot, w_unite, w_inner, w_outer, w_up):
    frames, chan, rows, cols = frame_feats.shape
    h = HALO
    m1 = inside_crop(rows, cols, h - 1)
    m2 = inside_crop(rows, cols, h - 2)
    w1 = w_unite.reshape(9, chan, 2 * chan)
    w2 = w_inner.reshape(9, chan, chan)
    w3 = w_outer.reshape(9, chan, chan)
    feats = frame_feats.transpose(0, 2, 1, 3)

    def finish(x_ext, w_first):
        padded = jnp.pad(x_ext, ((0, 0), (0, 0), (0, LANES - x_ext.shape[-1])))
        state, img = conv_chain(padded, m1, m2, w_first, w2, w3, w_up)
        image = img[:, :, :cols].transpose(1, 0, 2)
        return state[:, :, :cols], image

    state, first = finish(with_halo(feats[0], h), w1[:, :, chan:])

    def advance(state, inputs):
        feat, lists, slots = inputs
        warped = move_blocks(state, lists, slots)
        joined_ext = with_halo(jnp.concatenate([warped, feat], 1), h)
        return finish(joined_ext, w1)

    _, rest = lax.scan(advance, state, (feats[1:], send_list[1:, 0, 0], recv_slot[1:, 0, 0]))
    return jnp.concatenate([first[None], rest], 0)


def solution(mesh):
    placed = (
        P(None, None, "tile", "tm"),
        P(None, "tm", "tile", None, None),
        P(None, "tm", "tile", None),
        P(),
        P(),
        P(),
        P(),
    )
    return jax.shard_map(
        on_device,
        mesh=mesh,
        in_specs=placed,
        out_specs=P(None, None, "tile", "tm"),
        check_vma=False,
    )
```

```python
import jax
import jax.numpy as jnp
from jax import lax
from jax.sharding import PartitionSpec as P
from jax.experimental import pallas as pl
from jax.experimental.pallas import tpu as pltpu

HALO = 3


def shifted(value, moves):
    d_tm, d_tile = moves
    n_tm, n_tile = lax.axis_size("tm"), lax.axis_size("tile")
    pairs = []
    for a in range(n_tm):
        for b in range(n_tile):
            a2, b2 = a + d_tm, b + d_tile
            if 0 <= a2 < n_tm and 0 <= b2 < n_tile:
                pairs.append((a * n_tile + b, a2 * n_tile + b2))
    return lax.ppermute(value, ("tm", "tile"), pairs)


def with_halo(value, width):
    cols = value.shape[-1]
    west = shifted(value[..., :, cols - width :], (1, 0))
    east = shifted(value[..., :, :width], (-1, 0))
    middle = jnp.concatenate([west, value, east], -1)
    rows = middle.shape[-2]
    above = shifted(middle[..., rows - width :, :], (0, 1))
    below = shifted(middle[..., :width, :], (0, -1))
    return jnp.concatenate([above, middle, below], -2)


PITCH = 272


def flat_conv(src_ref, w_ref, out_rows):
    size = out_rows * PITCH
    total = None
    for b in range(3):
        part = None
        for a in range(3):
            term = jnp.dot(src_ref[a * PITCH : a * PITCH + size, :], w_ref[a * 3 + b],
                           preferred_element_type=jnp.float32)
            part = term if part is None else part + term
        if b:
            part = pltpu.roll(part, size - b, 0)
        total = part if total is None else total + part
    return total


def chain_kernel(x_ref, m1_ref, m2_ref, w1_ref, w2_ref, w3_ref, wup_ref, state_ref, img_ref, u_ref, i_ref):
    rows = state_ref.shape[0] // PITCH
    u_ref[...] = (flat_conv(x_ref, w1_ref, rows + 4) * m1_ref[...]).astype(jnp.bfloat16)
    inner = jnp.maximum(flat_conv(u_ref, w2_ref, rows + 2), 0.0)
    i_ref[...] = (inner * m2_ref[...]).astype(jnp.bfloat16)
    size = rows * PITCH
    res = pltpu.roll(u_ref[2 * PITCH : 2 * PITCH + size, :].astype(jnp.float32), size - 2, 0)
    st = (res + flat_conv(i_ref, w3_ref, rows)).astype(jnp.bfloat16)
    state_ref[...] = st
    img = lax.dot_general(wup_ref[...], st, (((1,), (1,)), ((), ())), preferred_element_type=jnp.float32)
    img_ref[...] = img.astype(jnp.bfloat16)


def conv_chain(x_flat, m1, m2, w1, w2, w3, wup, rows):
    chan, planes = w2.shape[1], wup.shape[0]
    return pl.pallas_call(
        chain_kernel,
        out_shape=(
            jax.ShapeDtypeStruct((rows * PITCH, chan), jnp.bfloat16),
            jax.ShapeDtypeStruct((planes, rows * PITCH), jnp.bfloat16),
        ),
        scratch_shapes=[
            pltpu.VMEM(((rows + 4) * PITCH, chan), jnp.bfloat16),
            pltpu.VMEM(((rows + 2) * PITCH, chan), jnp.bfloat16),
        ],
    )(x_flat, m1, m2, w1, w2, w3, wup)


def to_flat(x_ext):
    k, h, w = x_ext.shape
    hwc = jnp.pad(x_ext.transpose(1, 2, 0), ((0, 0), (0, PITCH - w), (0, 0)))
    return hwc.reshape(h * PITCH, k)


def inside_crop(rows, cols, margin):
    n_tm, n_tile = lax.axis_size("tm"), lax.axis_size("tile")
    band, strip = lax.axis_index("tile"), lax.axis_index("tm")
    r = band * rows - margin + jnp.arange(rows + 2 * margin, dtype=jnp.int32)
    x = jnp.arange(PITCH, dtype=jnp.int32)
    c = strip * cols - margin + x
    ok_r = (r >= 0) & (r < rows * n_tile)
    ok_c = (c >= 0) & (c < cols * n_tm) & (x < cols + 2 * margin)
    return (ok_r[:, None] & ok_c[None, :]).astype(jnp.float32).reshape(-1, 1)


def from_behind(value, axis, by):
    size = lax.axis_size(axis)
    pairs = [(i, i + by) for i in range(size) if 0 <= i + by < size]
    return lax.ppermute(value, axis, pairs)


def block_onehot(rows_of, cols_of, blk):
    pick = rows_of[:, None] == cols_of[None, :]
    eye = jnp.arange(blk)[:, None] == jnp.arange(blk)[None, :]
    full = pick[:, None, :, None] & eye[None, :, None, :]
    return full.reshape(rows_of.shape[0] * blk, cols_of.shape[0] * blk).astype(jnp.bfloat16)


def move_blocks(state, lists, slots):
    chan, rows, cols = state.shape
    entries = lists.shape[1]
    width = entries * rows
    blocks = cols // rows
    flat = state.reshape(chan * rows, cols)
    picker = block_onehot(jnp.arange(blocks, dtype=jnp.int32), lists.reshape(-1), rows)
    offered = jnp.dot(flat, picker, preferred_element_type=jnp.float32).astype(jnp.bfloat16)
    outgoing = [offered[:, offset * width : (offset + 1) * width] for offset in range(3)]
    pieces = []
    for offset in range(3):
        if offset == 1:
            pieces.append(outgoing[1])
        else:
            pieces.append(from_behind(outgoing[offset], "tile", 1 - offset))
    pool = jnp.concatenate(pieces, 1)
    placer = block_onehot(jnp.arange(3 * entries, dtype=jnp.int32), slots, rows)
    warped = jnp.dot(pool, placer, preferred_element_type=jnp.float32).astype(jnp.bfloat16)
    return warped.reshape(chan, rows, cols)


def on_device(frame_feats, send_list, recv_slot, w_unite, w_inner, w_outer, w_up):
    frames, chan, rows, cols = frame_feats.shape
    h = HALO
    m1 = inside_crop(rows, cols, h - 1)
    m2 = inside_crop(rows, cols, h - 2)
    w1 = w_unite.transpose(0, 1, 3, 2).reshape(9, 2 * chan, chan)
    w2 = w_inner.transpose(0, 1, 3, 2).reshape(9, chan, chan)
    w3 = w_outer.transpose(0, 1, 3, 2).reshape(9, chan, chan)

    def finish(x_ext, w_first):
        st, img = conv_chain(to_flat(x_ext), m1, m2, w_first, w2, w3, w_up, rows)
        state = st.reshape(rows, PITCH, chan)[:, :cols, :].transpose(2, 0, 1)
        image = img.reshape(w_up.shape[0], rows, PITCH)[:, :, :cols]
        return state, image

    state, first = finish(with_halo(frame_feats[0], h), w1[:, chan:, :])

    def advance(state, inputs):
        feats, lists, slots = inputs
        warped = move_blocks(state, lists, slots)
        joined_ext = with_halo(jnp.concatenate([warped, feats], 0), h)
        return finish(joined_ext, w1)

    _, rest = lax.scan(
        advance, state, (frame_feats[1:], send_list[1:, 0, 0], recv_slot[1:, 0, 0])
    )
    return jnp.concatenate([first[None], rest], 0)


def solution(mesh):
    placed = (
        P(None, None, "tile", "tm"),
        P(None, "tm", "tile", None, None),
        P(None, "tm", "tile", None),
        P(),
        P(),
        P(),
        P(),
    )
    return jax.shard_map(
        on_device,
        mesh=mesh,
        in_specs=placed,
        out_specs=P(None, None, "tile", "tm"),
        check_vma=False,
    )
```

```python
import jax
import jax.numpy as jnp
from jax import lax
from jax.sharding import PartitionSpec as P
from jax.experimental import pallas as pl
from jax.experimental.pallas import tpu as pltpu

HALO = 3


def shifted(value, moves):
    d_tm, d_tile = moves
    n_tm, n_tile = lax.axis_size("tm"), lax.axis_size("tile")
    pairs = []
    for a in range(n_tm):
        for b in range(n_tile):
            a2, b2 = a + d_tm, b + d_tile
            if 0 <= a2 < n_tm and 0 <= b2 < n_tile:
                pairs.append((a * n_tile + b, a2 * n_tile + b2))
    return lax.ppermute(value, ("tm", "tile"), pairs)


def with_halo(value, width):
    cols = value.shape[-1]
    west = shifted(value[..., :, cols - width :], (1, 0))
    east = shifted(value[..., :, :width], (-1, 0))
    middle = jnp.concatenate([west, value, east], -1)
    rows = middle.shape[-2]
    above = shifted(middle[..., rows - width :, :], (0, 1))
    below = shifted(middle[..., :width, :], (0, -1))
    return jnp.concatenate([above, middle, below], -2)


PITCH = 272


def flat_conv(src_ref, w_ref, out_rows):
    size = out_rows * PITCH
    total = None
    for b in range(3):
        part = None
        for a in range(3):
            term = jnp.dot(src_ref[a * PITCH : a * PITCH + size, :], w_ref[a * 3 + b],
                           preferred_element_type=jnp.float32)
            part = term if part is None else part + term
        if b:
            part = pltpu.roll(part, size - b, 0)
        total = part if total is None else total + part
    return total


def chain_kernel(x_ref, m1_ref, m2_ref, w1_ref, w2_ref, w3_ref, wup_ref, state_ref, img_ref, u_ref, i_ref):
    rows = state_ref.shape[0] // PITCH
    u_ref[...] = (flat_conv(x_ref, w1_ref, rows + 4) * m1_ref[...]).astype(jnp.bfloat16)
    inner = jnp.maximum(flat_conv(u_ref, w2_ref, rows + 2), 0.0)
    i_ref[...] = (inner * m2_ref[...]).astype(jnp.bfloat16)
    size = rows * PITCH
    res = pltpu.roll(u_ref[2 * PITCH : 2 * PITCH + size, :].astype(jnp.float32), size - 2, 0)
    st = (res + flat_conv(i_ref, w3_ref, rows)).astype(jnp.bfloat16)
    state_ref[...] = st
    img = lax.dot_general(wup_ref[...], st, (((1,), (1,)), ((), ())), preferred_element_type=jnp.float32)
    img_ref[...] = img.astype(jnp.bfloat16)


def conv_chain(x_flat, m1, m2, w1, w2, w3, wup, rows):
    chan, planes = w2.shape[1], wup.shape[0]
    return pl.pallas_call(
        chain_kernel,
        out_shape=(
            jax.ShapeDtypeStruct((rows * PITCH, chan), jnp.bfloat16),
            jax.ShapeDtypeStruct((planes, rows * PITCH), jnp.bfloat16),
        ),
        scratch_shapes=[
            pltpu.VMEM(((rows + 4) * PITCH, chan), jnp.bfloat16),
            pltpu.VMEM(((rows + 2) * PITCH, chan), jnp.bfloat16),
        ],
    )(x_flat, m1, m2, w1, w2, w3, wup)


def to_flat(x_ext):
    k, h, w = x_ext.shape
    hwc = jnp.pad(x_ext.transpose(1, 2, 0), ((0, 0), (0, PITCH - w), (0, 0)))
    return hwc.reshape(h * PITCH, k)


def inside_crop(rows, cols, margin):
    n_tm, n_tile = lax.axis_size("tm"), lax.axis_size("tile")
    band, strip = lax.axis_index("tile"), lax.axis_index("tm")
    r = band * rows - margin + jnp.arange(rows + 2 * margin, dtype=jnp.int32)
    x = jnp.arange(PITCH, dtype=jnp.int32)
    c = strip * cols - margin + x
    ok_r = (r >= 0) & (r < rows * n_tile)
    ok_c = (c >= 0) & (c < cols * n_tm) & (x < cols + 2 * margin)
    return (ok_r[:, None] & ok_c[None, :]).astype(jnp.float32).reshape(-1, 1)


def from_behind(value, axis, by):
    size = lax.axis_size(axis)
    pairs = [(i, i + by) for i in range(size) if 0 <= i + by < size]
    return lax.ppermute(value, axis, pairs)


def block_onehot(rows_of, cols_of, blk):
    pick = rows_of[:, None] == cols_of[None, :]
    eye = jnp.arange(blk)[:, None] == jnp.arange(blk)[None, :]
    full = pick[:, None, :, None] & eye[None, :, None, :]
    return full.reshape(rows_of.shape[0] * blk, cols_of.shape[0] * blk).astype(jnp.bfloat16)


def move_blocks(state, lists, slots):
    chan, rows, cols = state.shape
    entries = lists.shape[1]
    width = entries * rows
    blocks = cols // rows
    flat = state.reshape(chan * rows, cols)
    picker = block_onehot(jnp.arange(blocks, dtype=jnp.int32), lists.reshape(-1), rows)
    offered = jnp.dot(flat, picker, preferred_element_type=jnp.float32).astype(jnp.bfloat16)
    outgoing = [offered[:, offset * width : (offset + 1) * width] for offset in range(3)]
    pieces = []
    for offset in range(3):
        if offset == 1:
            pieces.append(outgoing[1])
        else:
            pieces.append(from_behind(outgoing[offset], "tile", 1 - offset))
    pool = jnp.concatenate(pieces, 1)
    placer = block_onehot(jnp.arange(3 * entries, dtype=jnp.int32), slots, rows)
    warped = jnp.dot(pool, placer, preferred_element_type=jnp.float32).astype(jnp.bfloat16)
    return warped.reshape(chan, rows, cols)


def on_device(frame_feats, send_list, recv_slot, w_unite, w_inner, w_outer, w_up):
    frames, chan, rows, cols = frame_feats.shape
    h = HALO
    m1 = jnp.broadcast_to(inside_crop(rows, cols, h - 1), ((rows + 4) * PITCH, chan)).astype(jnp.bfloat16)
    m2 = jnp.broadcast_to(inside_crop(rows, cols, h - 2), ((rows + 2) * PITCH, chan)).astype(jnp.bfloat16)
    w1 = w_unite.transpose(0, 1, 3, 2).reshape(9, 2 * chan, chan)
    w2 = w_inner.transpose(0, 1, 3, 2).reshape(9, chan, chan)
    w3 = w_outer.transpose(0, 1, 3, 2).reshape(9, chan, chan)

    def finish(x_ext, w_first):
        st, img = conv_chain(to_flat(x_ext), m1, m2, w_first, w2, w3, w_up, rows)
        state = st.reshape(rows, PITCH, chan)[:, :cols, :].transpose(2, 0, 1)
        image = img.reshape(w_up.shape[0], rows, PITCH)[:, :, :cols]
        return state, image

    state, first = finish(with_halo(frame_feats[0], h), w1[:, chan:, :])

    def advance(state, inputs):
        feats, lists, slots = inputs
        warped = move_blocks(state, lists, slots)
        joined_ext = with_halo(jnp.concatenate([warped, feats], 0), h)
        return finish(joined_ext, w1)

    _, rest = lax.scan(
        advance, state, (frame_feats[1:], send_list[1:, 0, 0], recv_slot[1:, 0, 0])
    )
    return jnp.concatenate([first[None], rest], 0)


def solution(mesh):
    placed = (
        P(None, None, "tile", "tm"),
        P(None, "tm", "tile", None, None),
        P(None, "tm", "tile", None),
        P(),
        P(),
        P(),
        P(),
    )
    return jax.shard_map(
        on_device,
        mesh=mesh,
        in_specs=placed,
        out_specs=P(None, None, "tile", "tm"),
        check_vma=False,
    )
```

```python
import jax
import jax.numpy as jnp
from jax import lax
from jax.sharding import PartitionSpec as P
from jax.experimental import pallas as pl
from jax.experimental.pallas import tpu as pltpu

HALO = 3


def shifted(value, moves):
    d_tm, d_tile = moves
    n_tm, n_tile = lax.axis_size("tm"), lax.axis_size("tile")
    pairs = []
    for a in range(n_tm):
        for b in range(n_tile):
            a2, b2 = a + d_tm, b + d_tile
            if 0 <= a2 < n_tm and 0 <= b2 < n_tile:
                pairs.append((a * n_tile + b, a2 * n_tile + b2))
    return lax.ppermute(value, ("tm", "tile"), pairs)


def with_halo(value, width):
    cols = value.shape[-1]
    west = shifted(value[..., :, cols - width :], (1, 0))
    east = shifted(value[..., :, :width], (-1, 0))
    middle = jnp.concatenate([west, value, east], -1)
    rows = middle.shape[-2]
    above = shifted(middle[..., rows - width :, :], (0, 1))
    below = shifted(middle[..., :width, :], (0, -1))
    return jnp.concatenate([above, middle, below], -2)


PITCH = 272


def flat_conv(src_ref, w_ref, out_rows):
    size = out_rows * PITCH
    total = None
    for b in range(3):
        part = None
        for a in range(3):
            term = jnp.dot(src_ref[a * PITCH : a * PITCH + size, :], w_ref[a * 3 + b],
                           preferred_element_type=jnp.float32)
            part = term if part is None else part + term
        if b:
            part = pltpu.roll(part, size - b, 0)
        total = part if total is None else total + part
    return total


def chain_kernel(x_ref, m1_ref, m2_ref, w1_ref, w2_ref, w3_ref, wup_ref, state_ref, img_ref, u_ref, i_ref):
    rows = state_ref.shape[0] // PITCH
    u_ref[...] = (flat_conv(x_ref, w1_ref, rows + 4) * m1_ref[...]).astype(jnp.bfloat16)
    inner = jnp.maximum(flat_conv(u_ref, w2_ref, rows + 2), 0.0)
    i_ref[...] = (inner * m2_ref[...]).astype(jnp.bfloat16)
    size = rows * PITCH
    res = pltpu.roll(u_ref[2 * PITCH : 2 * PITCH + size, :].astype(jnp.float32), size - 2, 0)
    st = (res + flat_conv(i_ref, w3_ref, rows)).astype(jnp.bfloat16)
    state_ref[...] = st
    img = lax.dot_general(wup_ref[...], st, (((1,), (1,)), ((), ())), preferred_element_type=jnp.float32)
    img_ref[...] = img.astype(jnp.bfloat16)


def conv_chain(x_flat, m1, m2, w1, w2, w3, wup, rows):
    chan, planes = w2.shape[1], wup.shape[0]
    return pl.pallas_call(
        chain_kernel,
        out_shape=(
            jax.ShapeDtypeStruct((rows * PITCH, chan), jnp.bfloat16),
            jax.ShapeDtypeStruct((planes, rows * PITCH), jnp.bfloat16),
        ),
        scratch_shapes=[
            pltpu.VMEM(((rows + 4) * PITCH, chan), jnp.bfloat16),
            pltpu.VMEM(((rows + 2) * PITCH, chan), jnp.bfloat16),
        ],
    )(x_flat, m1, m2, w1, w2, w3, wup)


def to_flat(x_ext):
    k, h, w = x_ext.shape
    hwc = jnp.pad(x_ext.transpose(1, 2, 0), ((0, 0), (0, PITCH - w), (0, 0)))
    return hwc.reshape(h * PITCH, k)


def inside_crop(rows, cols, margin):
    n_tm, n_tile = lax.axis_size("tm"), lax.axis_size("tile")
    band, strip = lax.axis_index("tile"), lax.axis_index("tm")
    r = band * rows - margin + jnp.arange(rows + 2 * margin, dtype=jnp.int32)
    x = jnp.arange(PITCH, dtype=jnp.int32)
    c = strip * cols - margin + x
    ok_r = (r >= 0) & (r < rows * n_tile)
    ok_c = (c >= 0) & (c < cols * n_tm) & (x < cols + 2 * margin)
    return (ok_r[:, None] & ok_c[None, :]).astype(jnp.float32).reshape(-1, 1)


def from_behind(value, axis, by):
    size = lax.axis_size(axis)
    pairs = [(i, i + by) for i in range(size) if 0 <= i + by < size]
    return lax.ppermute(value, axis, pairs)


def block_onehot(rows_of, cols_of, blk):
    pick = rows_of[:, None] == cols_of[None, :]
    eye = jnp.arange(blk)[:, None] == jnp.arange(blk)[None, :]
    full = pick[:, None, :, None] & eye[None, :, None, :]
    return full.reshape(rows_of.shape[0] * blk, cols_of.shape[0] * blk).astype(jnp.bfloat16)


def move_blocks(state, lists, slots):
    chan, rows, cols = state.shape
    entries = lists.shape[1]
    width = entries * rows
    blocks = cols // rows
    flat = state.reshape(chan * rows, cols)
    picker = block_onehot(jnp.arange(blocks, dtype=jnp.int32), lists.reshape(-1), rows)
    offered = jnp.dot(flat, picker, preferred_element_type=jnp.float32).astype(jnp.bfloat16)
    outgoing = [offered[:, offset * width : (offset + 1) * width] for offset in range(3)]
    pieces = []
    for offset in range(3):
        if offset == 1:
            pieces.append(outgoing[1])
        else:
            pieces.append(from_behind(outgoing[offset], "tile", 1 - offset))
    pool = jnp.concatenate(pieces, 1)
    placer = block_onehot(jnp.arange(3 * entries, dtype=jnp.int32), slots, rows)
    warped = jnp.dot(pool, placer, preferred_element_type=jnp.float32).astype(jnp.bfloat16)
    return warped.reshape(chan, rows, cols)


def on_device(frame_feats, send_list, recv_slot, w_unite, w_inner, w_outer, w_up):
    frames, chan, rows, cols = frame_feats.shape
    h = HALO
    m1 = jnp.broadcast_to(inside_crop(rows, cols, h - 1), ((rows + 4) * PITCH, chan)).astype(jnp.bfloat16)
    m2 = jnp.broadcast_to(inside_crop(rows, cols, h - 2), ((rows + 2) * PITCH, chan)).astype(jnp.bfloat16)
    m1, m2 = lax.optimization_barrier((m1, m2))
    w1 = w_unite.transpose(0, 1, 3, 2).reshape(9, 2 * chan, chan)
    w2 = w_inner.transpose(0, 1, 3, 2).reshape(9, chan, chan)
    w3 = w_outer.transpose(0, 1, 3, 2).reshape(9, chan, chan)

    def finish(x_ext, w_first):
        st, img = conv_chain(to_flat(x_ext), m1, m2, w_first, w2, w3, w_up, rows)
        state = st.reshape(rows, PITCH, chan)[:, :cols, :].transpose(2, 0, 1)
        image = img.reshape(w_up.shape[0], rows, PITCH)[:, :, :cols]
        return state, image

    state, first = finish(with_halo(frame_feats[0], h), w1[:, chan:, :])

    def advance(state, inputs):
        feats, lists, slots = inputs
        warped = move_blocks(state, lists, slots)
        joined_ext = with_halo(jnp.concatenate([warped, feats], 0), h)
        return finish(joined_ext, w1)

    _, rest = lax.scan(
        advance, state, (frame_feats[1:], send_list[1:, 0, 0], recv_slot[1:, 0, 0])
    )
    return jnp.concatenate([first[None], rest], 0)


def solution(mesh):
    placed = (
        P(None, None, "tile", "tm"),
        P(None, "tm", "tile", None, None),
        P(None, "tm", "tile", None),
        P(),
        P(),
        P(),
        P(),
    )
    return jax.shard_map(
        on_device,
        mesh=mesh,
        in_specs=placed,
        out_specs=P(None, None, "tile", "tm"),
        check_vma=False,
    )
```

```python
import jax
import jax.numpy as jnp
from jax import lax
from jax.sharding import PartitionSpec as P
from jax.experimental import pallas as pl
from jax.experimental.pallas import tpu as pltpu

HALO = 3


def shifted(value, moves):
    d_tm, d_tile = moves
    n_tm, n_tile = lax.axis_size("tm"), lax.axis_size("tile")
    pairs = []
    for a in range(n_tm):
        for b in range(n_tile):
            a2, b2 = a + d_tm, b + d_tile
            if 0 <= a2 < n_tm and 0 <= b2 < n_tile:
                pairs.append((a * n_tile + b, a2 * n_tile + b2))
    return lax.ppermute(value, ("tm", "tile"), pairs)


def with_halo(value, width):
    cols = value.shape[-1]
    west = shifted(value[..., :, cols - width :], (1, 0))
    east = shifted(value[..., :, :width], (-1, 0))
    middle = jnp.concatenate([west, value, east], -1)
    rows = middle.shape[-2]
    above = shifted(middle[..., rows - width :, :], (0, 1))
    below = shifted(middle[..., :width, :], (0, -1))
    return jnp.concatenate([above, middle, below], -2)


PITCH = 272


def flat_conv(src_ref, w_ref, out_rows):
    size = out_rows * PITCH
    total = None
    for b in range(3):
        part = None
        for a in range(3):
            term = jnp.dot(src_ref[a * PITCH : a * PITCH + size, :], w_ref[a * 3 + b],
                           preferred_element_type=jnp.float32)
            part = term if part is None else part + term
        if b:
            part = pltpu.roll(part, size - b, 0)
        total = part if total is None else total + part
    return total


def crop_mask(org_ref, out_rows, margin, chan):
    y = lax.broadcasted_iota(jnp.int32, (out_rows, PITCH, chan), 0)
    x = lax.broadcasted_iota(jnp.int32, (out_rows, PITCH, chan), 1)
    r = org_ref[0] - margin + y
    c = org_ref[1] - margin + x
    width = org_ref[4]
    ok = (r >= 0) & (r < org_ref[2]) & (c >= 0) & (c < org_ref[3]) & (x < width + 2 * margin)
    return ok.astype(jnp.float32)


def masked(acc, mask):
    rows = mask.shape[0]
    return (acc.reshape(rows, PITCH, acc.shape[-1]) * mask).reshape(acc.shape)


def chain_kernel(org_ref, x_ref, w1_ref, w2_ref, w3_ref, wup_ref, state_ref, img_ref, u_ref, i_ref):
    rows = state_ref.shape[0] // PITCH
    chan = state_ref.shape[1]
    m1 = crop_mask(org_ref, rows + 4, 2, chan)
    u_ref[...] = masked(flat_conv(x_ref, w1_ref, rows + 4), m1).astype(jnp.bfloat16)
    m2 = crop_mask(org_ref, rows + 2, 1, chan)
    inner = jnp.maximum(flat_conv(u_ref, w2_ref, rows + 2), 0.0)
    i_ref[...] = masked(inner, m2).astype(jnp.bfloat16)
    size = rows * PITCH
    res = pltpu.roll(u_ref[2 * PITCH : 2 * PITCH + size, :].astype(jnp.float32), size - 2, 0)
    st = (res + flat_conv(i_ref, w3_ref, rows)).astype(jnp.bfloat16)
    state_ref[...] = st
    img = lax.dot_general(wup_ref[...], st, (((1,), (1,)), ((), ())), preferred_element_type=jnp.float32)
    img_ref[...] = img.astype(jnp.bfloat16)


def conv_chain(origin, x_flat, w1, w2, w3, wup, rows):
    chan, planes = w2.shape[1], wup.shape[0]
    vmem = pl.BlockSpec(memory_space=pltpu.VMEM)
    return pl.pallas_call(
        chain_kernel,
        out_shape=(
            jax.ShapeDtypeStruct((rows * PITCH, chan), jnp.bfloat16),
            jax.ShapeDtypeStruct((planes, rows * PITCH), jnp.bfloat16),
        ),
        in_specs=[pl.BlockSpec(memory_space=pltpu.SMEM)] + [vmem] * 5,
        out_specs=(vmem, vmem),
        scratch_shapes=[
            pltpu.VMEM(((rows + 4) * PITCH, chan), jnp.bfloat16),
            pltpu.VMEM(((rows + 2) * PITCH, chan), jnp.bfloat16),
        ],
    )(origin, x_flat, w1, w2, w3, wup)


def to_flat(x_ext):
    k, h, w = x_ext.shape
    hwc = jnp.pad(x_ext.transpose(1, 2, 0), ((0, 0), (0, PITCH - w), (0, 0)))
    return hwc.reshape(h * PITCH, k)


def tile_origin(rows, cols):
    n_tm, n_tile = lax.axis_size("tm"), lax.axis_size("tile")
    band, strip = lax.axis_index("tile"), lax.axis_index("tm")
    return jnp.stack([band * rows, strip * cols, jnp.int32(rows * n_tile), jnp.int32(cols * n_tm), jnp.int32(cols)]).astype(jnp.int32)


def from_behind(value, axis, by):
    size = lax.axis_size(axis)
    pairs = [(i, i + by) for i in range(size) if 0 <= i + by < size]
    return lax.ppermute(value, axis, pairs)


def block_onehot(rows_of, cols_of, blk):
    pick = rows_of[:, None] == cols_of[None, :]
    eye = jnp.arange(blk)[:, None] == jnp.arange(blk)[None, :]
    full = pick[:, None, :, None] & eye[None, :, None, :]
    return full.reshape(rows_of.shape[0] * blk, cols_of.shape[0] * blk).astype(jnp.bfloat16)


def move_blocks(state, lists, slots):
    chan, rows, cols = state.shape
    entries = lists.shape[1]
    width = entries * rows
    blocks = cols // rows
    flat = state.reshape(chan * rows, cols)
    picker = block_onehot(jnp.arange(blocks, dtype=jnp.int32), lists.reshape(-1), rows)
    offered = jnp.dot(flat, picker, preferred_element_type=jnp.float32).astype(jnp.bfloat16)
    outgoing = [offered[:, offset * width : (offset + 1) * width] for offset in range(3)]
    pieces = []
    for offset in range(3):
        if offset == 1:
            pieces.append(outgoing[1])
        else:
            pieces.append(from_behind(outgoing[offset], "tile", 1 - offset))
    pool = jnp.concatenate(pieces, 1)
    placer = block_onehot(jnp.arange(3 * entries, dtype=jnp.int32), slots, rows)
    warped = jnp.dot(pool, placer, preferred_element_type=jnp.float32).astype(jnp.bfloat16)
    return warped.reshape(chan, rows, cols)


def on_device(frame_feats, send_list, recv_slot, w_unite, w_inner, w_outer, w_up):
    frames, chan, rows, cols = frame_feats.shape
    h = HALO
    origin = tile_origin(rows, cols)
    w1 = w_unite.transpose(0, 1, 3, 2).reshape(9, 2 * chan, chan)
    w2 = w_inner.transpose(0, 1, 3, 2).reshape(9, chan, chan)
    w3 = w_outer.transpose(0, 1, 3, 2).reshape(9, chan, chan)

    def finish(x_ext, w_first):
        st, img = conv_chain(origin, to_flat(x_ext), w_first, w2, w3, w_up, rows)
        state = st.reshape(rows, PITCH, chan)[:, :cols, :].transpose(2, 0, 1)
        image = img.reshape(w_up.shape[0], rows, PITCH)[:, :, :cols]
        return state, image

    state, first = finish(with_halo(frame_feats[0], h), w1[:, chan:, :])

    def advance(state, inputs):
        feats, lists, slots = inputs
        warped = move_blocks(state, lists, slots)
        joined_ext = with_halo(jnp.concatenate([warped, feats], 0), h)
        return finish(joined_ext, w1)

    _, rest = lax.scan(
        advance, state, (frame_feats[1:], send_list[1:, 0, 0], recv_slot[1:, 0, 0])
    )
    return jnp.concatenate([first[None], rest], 0)


def solution(mesh):
    placed = (
        P(None, None, "tile", "tm"),
        P(None, "tm", "tile", None, None),
        P(None, "tm", "tile", None),
        P(),
        P(),
        P(),
        P(),
    )
    return jax.shard_map(
        on_device,
        mesh=mesh,
        in_specs=placed,
        out_specs=P(None, None, "tile", "tm"),
        check_vma=False,
    )
```

```python
import jax
import jax.numpy as jnp
from jax import lax
from jax.sharding import PartitionSpec as P
from jax.experimental import pallas as pl
from jax.experimental.pallas import tpu as pltpu

HALO = 3


def shifted(value, moves):
    d_tm, d_tile = moves
    n_tm, n_tile = lax.axis_size("tm"), lax.axis_size("tile")
    pairs = []
    for a in range(n_tm):
        for b in range(n_tile):
            a2, b2 = a + d_tm, b + d_tile
            if 0 <= a2 < n_tm and 0 <= b2 < n_tile:
                pairs.append((a * n_tile + b, a2 * n_tile + b2))
    return lax.ppermute(value, ("tm", "tile"), pairs)


def with_halo(value, width, pitch=None):
    cols = value.shape[-1]
    west = shifted(value[..., :, cols - width :], (1, 0))
    east = shifted(value[..., :, :width], (-1, 0))
    pieces = [west, value, east]
    if pitch is not None and pitch > cols + 2 * width:
        pieces.append(jnp.zeros(value.shape[:-1] + (pitch - cols - 2 * width,), value.dtype))
    middle = jnp.concatenate(pieces, -1)
    rows = middle.shape[-2]
    above = shifted(middle[..., rows - width :, :], (0, 1))
    below = shifted(middle[..., :width, :], (0, -1))
    return jnp.concatenate([above, middle, below], -2)


PITCH = 272


def flat_conv(src_ref, w_ref, out_rows):
    size = out_rows * PITCH
    total = None
    for b in range(3):
        part = None
        for a in range(3):
            term = jnp.dot(src_ref[a * PITCH : a * PITCH + size, :], w_ref[a * 3 + b],
                           preferred_element_type=jnp.float32)
            part = term if part is None else part + term
        if b:
            part = pltpu.roll(part, size - b, 0)
        total = part if total is None else total + part
    return total


def crop_mask(org_ref, out_rows, margin, chan):
    y = lax.broadcasted_iota(jnp.int32, (out_rows, PITCH, chan), 0)
    x = lax.broadcasted_iota(jnp.int32, (out_rows, PITCH, chan), 1)
    r = org_ref[0] - margin + y
    c = org_ref[1] - margin + x
    width = org_ref[4]
    ok = (r >= 0) & (r < org_ref[2]) & (c >= 0) & (c < org_ref[3]) & (x < width + 2 * margin)
    return ok.astype(jnp.float32)


def masked(acc, mask):
    rows = mask.shape[0]
    return (acc.reshape(rows, PITCH, acc.shape[-1]) * mask).reshape(acc.shape)


def chain_kernel(org_ref, x_ref, w1_ref, w2_ref, w3_ref, wup_ref, state_ref, img_ref, u_ref, i_ref):
    rows = state_ref.shape[0] // PITCH
    chan = state_ref.shape[1]
    m1 = crop_mask(org_ref, rows + 4, 2, chan)
    u_ref[...] = masked(flat_conv(x_ref, w1_ref, rows + 4), m1).astype(jnp.bfloat16)
    m2 = crop_mask(org_ref, rows + 2, 1, chan)
    inner = jnp.maximum(flat_conv(u_ref, w2_ref, rows + 2), 0.0)
    i_ref[...] = masked(inner, m2).astype(jnp.bfloat16)
    size = rows * PITCH
    res = pltpu.roll(u_ref[2 * PITCH : 2 * PITCH + size, :].astype(jnp.float32), size - 2, 0)
    st = (res + flat_conv(i_ref, w3_ref, rows)).astype(jnp.bfloat16)
    state_ref[...] = st
    img = lax.dot_general(wup_ref[...], st, (((1,), (1,)), ((), ())), preferred_element_type=jnp.float32)
    img_ref[...] = img.astype(jnp.bfloat16)


def conv_chain(origin, x_flat, w1, w2, w3, wup, rows):
    chan, planes = w2.shape[1], wup.shape[0]
    vmem = pl.BlockSpec(memory_space=pltpu.VMEM)
    return pl.pallas_call(
        chain_kernel,
        out_shape=(
            jax.ShapeDtypeStruct((rows * PITCH, chan), jnp.bfloat16),
            jax.ShapeDtypeStruct((planes, rows * PITCH), jnp.bfloat16),
        ),
        in_specs=[pl.BlockSpec(memory_space=pltpu.SMEM)] + [vmem] * 5,
        out_specs=(vmem, vmem),
        scratch_shapes=[
            pltpu.VMEM(((rows + 4) * PITCH, chan), jnp.bfloat16),
            pltpu.VMEM(((rows + 2) * PITCH, chan), jnp.bfloat16),
        ],
    )(origin, x_flat, w1, w2, w3, wup)


def to_flat(x_ext):
    k, h, w = x_ext.shape
    hwc = x_ext.transpose(1, 2, 0)
    return hwc.reshape(h * PITCH, k)


def tile_origin(rows, cols):
    n_tm, n_tile = lax.axis_size("tm"), lax.axis_size("tile")
    band, strip = lax.axis_index("tile"), lax.axis_index("tm")
    return jnp.stack([band * rows, strip * cols, jnp.int32(rows * n_tile), jnp.int32(cols * n_tm), jnp.int32(cols)]).astype(jnp.int32)


def from_behind(value, axis, by):
    size = lax.axis_size(axis)
    pairs = [(i, i + by) for i in range(size) if 0 <= i + by < size]
    return lax.ppermute(value, axis, pairs)


def block_onehot(rows_of, cols_of, blk):
    pick = rows_of[:, None] == cols_of[None, :]
    eye = jnp.arange(blk)[:, None] == jnp.arange(blk)[None, :]
    full = pick[:, None, :, None] & eye[None, :, None, :]
    return full.reshape(rows_of.shape[0] * blk, cols_of.shape[0] * blk).astype(jnp.bfloat16)


def move_blocks(state, lists, slots):
    chan, rows, cols = state.shape
    entries = lists.shape[1]
    width = entries * rows
    blocks = cols // rows
    flat = state.reshape(chan * rows, cols)
    picker = block_onehot(jnp.arange(blocks, dtype=jnp.int32), lists.reshape(-1), rows)
    offered = jnp.dot(flat, picker, preferred_element_type=jnp.float32).astype(jnp.bfloat16)
    outgoing = [offered[:, offset * width : (offset + 1) * width] for offset in range(3)]
    pieces = []
    for offset in range(3):
        if offset == 1:
            pieces.append(outgoing[1])
        else:
            pieces.append(from_behind(outgoing[offset], "tile", 1 - offset))
    pool = jnp.concatenate(pieces, 1)
    placer = block_onehot(jnp.arange(3 * entries, dtype=jnp.int32), slots, rows)
    warped = jnp.dot(pool, placer, preferred_element_type=jnp.float32).astype(jnp.bfloat16)
    return warped.reshape(chan, rows, cols)


def on_device(frame_feats, send_list, recv_slot, w_unite, w_inner, w_outer, w_up):
    frames, chan, rows, cols = frame_feats.shape
    h = HALO
    origin = tile_origin(rows, cols)
    w1 = w_unite.transpose(0, 1, 3, 2).reshape(9, 2 * chan, chan)
    w2 = w_inner.transpose(0, 1, 3, 2).reshape(9, chan, chan)
    w3 = w_outer.transpose(0, 1, 3, 2).reshape(9, chan, chan)

    def finish(x_ext, w_first):
        st, img = conv_chain(origin, to_flat(x_ext), w_first, w2, w3, w_up, rows)
        state = st.reshape(rows, PITCH, chan)[:, :cols, :].transpose(2, 0, 1)
        image = img.reshape(w_up.shape[0], rows, PITCH)[:, :, :cols]
        return state, image

    state, first = finish(with_halo(frame_feats[0], h, PITCH), w1[:, chan:, :])

    def advance(state, inputs):
        feats, lists, slots = inputs
        warped = move_blocks(state, lists, slots)
        joined_ext = with_halo(jnp.concatenate([warped, feats], 0), h, PITCH)
        return finish(joined_ext, w1)

    _, rest = lax.scan(
        advance, state, (frame_feats[1:], send_list[1:, 0, 0], recv_slot[1:, 0, 0])
    )
    return jnp.concatenate([first[None], rest], 0)


def solution(mesh):
    placed = (
        P(None, None, "tile", "tm"),
        P(None, "tm", "tile", None, None),
        P(None, "tm", "tile", None),
        P(),
        P(),
        P(),
        P(),
    )
    return jax.shard_map(
        on_device,
        mesh=mesh,
        in_specs=placed,
        out_specs=P(None, None, "tile", "tm"),
        check_vma=False,
    )
```

```python
import jax
import jax.numpy as jnp
from jax import lax
from jax.sharding import PartitionSpec as P
from jax.experimental import pallas as pl
from jax.experimental.pallas import tpu as pltpu

HALO = 3


def shifted(value, moves):
    d_tm, d_tile = moves
    n_tm, n_tile = lax.axis_size("tm"), lax.axis_size("tile")
    pairs = []
    for a in range(n_tm):
        for b in range(n_tile):
            a2, b2 = a + d_tm, b + d_tile
            if 0 <= a2 < n_tm and 0 <= b2 < n_tile:
                pairs.append((a * n_tile + b, a2 * n_tile + b2))
    return lax.ppermute(value, ("tm", "tile"), pairs)


def with_halo(value, width):
    cols = value.shape[-1]
    west = shifted(value[..., :, cols - width :], (1, 0))
    east = shifted(value[..., :, :width], (-1, 0))
    middle = jnp.concatenate([west, value, east], -1)
    rows = middle.shape[-2]
    above = shifted(middle[..., rows - width :, :], (0, 1))
    below = shifted(middle[..., :width, :], (0, -1))
    return jnp.concatenate([above, middle, below], -2)


PITCH = 272


def flat_conv(src_ref, w_ref, out_rows):
    size = out_rows * PITCH
    total = None
    for b in range(3):
        part = None
        for a in range(3):
            term = jnp.dot(src_ref[a * PITCH : a * PITCH + size, :], w_ref[a * 3 + b],
                           preferred_element_type=jnp.float32)
            part = term if part is None else part + term
        if b:
            part = pltpu.roll(part, size - b, 0)
        total = part if total is None else total + part
    return total


def crop_mask(org_ref, out_rows, margin, chan):
    y = lax.broadcasted_iota(jnp.int32, (out_rows, PITCH, chan), 0)
    x = lax.broadcasted_iota(jnp.int32, (out_rows, PITCH, chan), 1)
    r = org_ref[0] - margin + y
    c = org_ref[1] - margin + x
    width = org_ref[4]
    ok = (r >= 0) & (r < org_ref[2]) & (c >= 0) & (c < org_ref[3]) & (x < width + 2 * margin)
    return ok.astype(jnp.float32)


def masked(acc, mask):
    rows = mask.shape[0]
    return (acc.reshape(rows, PITCH, acc.shape[-1]) * mask).reshape(acc.shape)


def chain_kernel(org_ref, x_ref, w1_ref, w2_ref, w3_ref, wup_ref, img_ref, u_ref, i_ref):
    rows = img_ref.shape[1] // PITCH
    chan = u_ref.shape[1]
    m1 = crop_mask(org_ref, rows + 4, 2, chan)
    u_ref[...] = masked(flat_conv(x_ref, w1_ref, rows + 4), m1).astype(jnp.bfloat16)
    m2 = crop_mask(org_ref, rows + 2, 1, chan)
    inner = jnp.maximum(flat_conv(u_ref, w2_ref, rows + 2), 0.0)
    i_ref[...] = masked(inner, m2).astype(jnp.bfloat16)
    size = rows * PITCH
    res = pltpu.roll(u_ref[2 * PITCH : 2 * PITCH + size, :].astype(jnp.float32), size - 2, 0)
    st = (res + flat_conv(i_ref, w3_ref, rows)).astype(jnp.bfloat16)
    img = lax.dot_general(wup_ref[...], st, (((1,), (1,)), ((), ())), preferred_element_type=jnp.float32)
    img_ref[...] = img.astype(jnp.bfloat16)


def conv_chain(origin, x_flat, w1, w2, w3, wup, rows):
    chan, planes = w2.shape[1], wup.shape[0]
    vmem = pl.BlockSpec(memory_space=pltpu.VMEM)
    return pl.pallas_call(
        chain_kernel,
        out_shape=jax.ShapeDtypeStruct((planes, rows * PITCH), jnp.bfloat16),
        in_specs=[pl.BlockSpec(memory_space=pltpu.SMEM)] + [vmem] * 5,
        out_specs=vmem,
        scratch_shapes=[
            pltpu.VMEM(((rows + 4) * PITCH, chan), jnp.bfloat16),
            pltpu.VMEM(((rows + 2) * PITCH, chan), jnp.bfloat16),
        ],
    )(origin, x_flat, w1, w2, w3, wup)


def to_flat(x_ext):
    k, h, w = x_ext.shape
    hwc = jnp.pad(x_ext.transpose(1, 2, 0), ((0, 0), (0, PITCH - w), (0, 0)))
    return hwc.reshape(h * PITCH, k)


def tile_origin(rows, cols):
    n_tm, n_tile = lax.axis_size("tm"), lax.axis_size("tile")
    band, strip = lax.axis_index("tile"), lax.axis_index("tm")
    return jnp.stack([band * rows, strip * cols, jnp.int32(rows * n_tile), jnp.int32(cols * n_tm), jnp.int32(cols)]).astype(jnp.int32)


def from_behind(value, axis, by):
    size = lax.axis_size(axis)
    pairs = [(i, i + by) for i in range(size) if 0 <= i + by < size]
    return lax.ppermute(value, axis, pairs)


def block_onehot(rows_of, cols_of, blk):
    pick = rows_of[:, None] == cols_of[None, :]
    eye = jnp.arange(blk)[:, None] == jnp.arange(blk)[None, :]
    full = pick[:, None, :, None] & eye[None, :, None, :]
    return full.reshape(rows_of.shape[0] * blk, cols_of.shape[0] * blk).astype(jnp.bfloat16)


def move_blocks(state, lists, slots):
    chan, rows, cols = state.shape
    entries = lists.shape[1]
    width = entries * rows
    blocks = cols // rows
    flat = state.reshape(chan * rows, cols)
    picker = block_onehot(jnp.arange(blocks, dtype=jnp.int32), lists.reshape(-1), rows)
    offered = jnp.dot(flat, picker, preferred_element_type=jnp.float32).astype(jnp.bfloat16)
    outgoing = [offered[:, offset * width : (offset + 1) * width] for offset in range(3)]
    pieces = []
    for offset in range(3):
        if offset == 1:
            pieces.append(outgoing[1])
        else:
            pieces.append(from_behind(outgoing[offset], "tile", 1 - offset))
    pool = jnp.concatenate(pieces, 1)
    placer = block_onehot(jnp.arange(3 * entries, dtype=jnp.int32), slots, rows)
    warped = jnp.dot(pool, placer, preferred_element_type=jnp.float32).astype(jnp.bfloat16)
    return warped.reshape(chan, rows, cols)


def on_device(frame_feats, send_list, recv_slot, w_unite, w_inner, w_outer, w_up):
    frames, chan, rows, cols = frame_feats.shape
    h = HALO
    origin = tile_origin(rows, cols)
    w1 = w_unite.transpose(0, 1, 3, 2).reshape(9, 2 * chan, chan)
    w2 = w_inner.transpose(0, 1, 3, 2).reshape(9, chan, chan)
    w3 = w_outer.transpose(0, 1, 3, 2).reshape(9, chan, chan)
    planes = w_up.shape[0]
    w_out = jnp.concatenate([w_up, jnp.eye(chan, dtype=w_up.dtype)], 0)

    def finish(x_ext, w_first):
        out = conv_chain(origin, to_flat(x_ext), w_first, w2, w3, w_out, rows)
        out = out.reshape(planes + chan, rows, PITCH)[:, :, :cols]
        state, image = out[planes:], out[:planes]
        return state, image

    state, first = finish(with_halo(frame_feats[0], h), w1[:, chan:, :])

    def advance(state, inputs):
        feats, lists, slots = inputs
        warped = move_blocks(state, lists, slots)
        joined_ext = with_halo(jnp.concatenate([warped, feats], 0), h)
        return finish(joined_ext, w1)

    _, rest = lax.scan(
        advance, state, (frame_feats[1:], send_list[1:, 0, 0], recv_slot[1:, 0, 0])
    )
    return jnp.concatenate([first[None], rest], 0)


def solution(mesh):
    placed = (
        P(None, None, "tile", "tm"),
        P(None, "tm", "tile", None, None),
        P(None, "tm", "tile", None),
        P(),
        P(),
        P(),
        P(),
    )
    return jax.shard_map(
        on_device,
        mesh=mesh,
        in_specs=placed,
        out_specs=P(None, None, "tile", "tm"),
        check_vma=False,
    )
```

```python
import jax
import jax.numpy as jnp
from jax import lax
from jax.sharding import PartitionSpec as P
from jax.experimental import pallas as pl
from jax.experimental.pallas import tpu as pltpu

HALO = 3


def shifted(value, moves):
    d_tm, d_tile = moves
    n_tm, n_tile = lax.axis_size("tm"), lax.axis_size("tile")
    pairs = []
    for a in range(n_tm):
        for b in range(n_tile):
            a2, b2 = a + d_tm, b + d_tile
            if 0 <= a2 < n_tm and 0 <= b2 < n_tile:
                pairs.append((a * n_tile + b, a2 * n_tile + b2))
    return lax.ppermute(value, ("tm", "tile"), pairs)


def with_halo(value, width):
    cols = value.shape[-1]
    west = shifted(value[..., :, cols - width :], (1, 0))
    east = shifted(value[..., :, :width], (-1, 0))
    middle = jnp.concatenate([west, value, east], -1)
    rows = middle.shape[-2]
    above = shifted(middle[..., rows - width :, :], (0, 1))
    below = shifted(middle[..., :width, :], (0, -1))
    return jnp.concatenate([above, middle, below], -2)


PITCH = 272


def flat_conv(src_ref, w_ref, out_rows):
    size = out_rows * PITCH
    total = None
    for b in range(3):
        part = None
        for a in range(3):
            term = jnp.dot(src_ref[a * PITCH : a * PITCH + size, :], w_ref[a * 3 + b],
                           preferred_element_type=jnp.float32)
            part = term if part is None else part + term
        if b:
            part = pltpu.roll(part, size - b, 0)
        total = part if total is None else total + part
    return total


def crop_mask(org_ref, out_rows, margin, chan):
    y = lax.broadcasted_iota(jnp.int32, (out_rows, PITCH, chan), 0)
    x = lax.broadcasted_iota(jnp.int32, (out_rows, PITCH, chan), 1)
    r = org_ref[0] - margin + y
    c = org_ref[1] - margin + x
    width = org_ref[4]
    ok = (r >= 0) & (r < org_ref[2]) & (c >= 0) & (c < org_ref[3]) & (x < width + 2 * margin)
    return ok.astype(jnp.float32)


def masked(acc, mask):
    rows = mask.shape[0]
    return (acc.reshape(rows, PITCH, acc.shape[-1]) * mask).reshape(acc.shape)


def chain_kernel(org_ref, x_ref, w1_ref, w2_ref, w3_ref, wup_ref, img_ref, u_ref, i_ref):
    rows = img_ref.shape[1] // PITCH
    chan = u_ref.shape[1]
    m1 = crop_mask(org_ref, rows + 4, 2, chan)
    u_ref[...] = masked(flat_conv(x_ref, w1_ref, rows + 4), m1).astype(jnp.bfloat16)
    m2 = crop_mask(org_ref, rows + 2, 1, chan)
    inner = jnp.maximum(flat_conv(u_ref, w2_ref, rows + 2), 0.0)
    i_ref[...] = masked(inner, m2).astype(jnp.bfloat16)
    size = rows * PITCH
    res = pltpu.roll(u_ref[2 * PITCH : 2 * PITCH + size, :].astype(jnp.float32), size - 2, 0)
    st = (res + flat_conv(i_ref, w3_ref, rows)).astype(jnp.bfloat16)
    img = lax.dot_general(wup_ref[...], st, (((1,), (1,)), ((), ())), preferred_element_type=jnp.float32)
    img_ref[...] = img.astype(jnp.bfloat16)


def conv_chain(origin, x_flat, w1, w2, w3, wup, rows):
    chan, planes = w2.shape[1], wup.shape[0]
    vmem = pl.BlockSpec(memory_space=pltpu.VMEM)
    return pl.pallas_call(
        chain_kernel,
        out_shape=jax.ShapeDtypeStruct((planes, rows * PITCH), jnp.bfloat16),
        in_specs=[pl.BlockSpec(memory_space=pltpu.SMEM)] + [vmem] * 5,
        out_specs=vmem,
        scratch_shapes=[
            pltpu.VMEM(((rows + 4) * PITCH, chan), jnp.bfloat16),
            pltpu.VMEM(((rows + 2) * PITCH, chan), jnp.bfloat16),
        ],
    )(origin, x_flat, w1, w2, w3, wup)


def to_flat(x_ext):
    k, h, w = x_ext.shape
    hwc = jnp.pad(x_ext.transpose(1, 2, 0), ((0, 0), (0, PITCH - w), (0, 0)))
    return hwc.reshape(h * PITCH, k)


def tile_origin(rows, cols):
    n_tm, n_tile = lax.axis_size("tm"), lax.axis_size("tile")
    band, strip = lax.axis_index("tile"), lax.axis_index("tm")
    return jnp.stack([band * rows, strip * cols, jnp.int32(rows * n_tile), jnp.int32(cols * n_tm), jnp.int32(cols)]).astype(jnp.int32)


def from_behind(value, axis, by):
    size = lax.axis_size(axis)
    pairs = [(i, i + by) for i in range(size) if 0 <= i + by < size]
    return lax.ppermute(value, axis, pairs)


def block_onehot(rows_of, cols_of, blk):
    pick = rows_of[:, None] == cols_of[None, :]
    eye = jnp.arange(blk)[:, None] == jnp.arange(blk)[None, :]
    full = pick[:, None, :, None] & eye[None, :, None, :]
    return full.reshape(rows_of.shape[0] * blk, cols_of.shape[0] * blk).astype(jnp.bfloat16)


def move_blocks(state, lists, slots):
    chan, rows, cols = state.shape
    entries = lists.shape[1]
    width = entries * rows
    blocks = cols // rows
    flat = state.reshape(chan * rows, cols)
    picker = block_onehot(jnp.arange(blocks, dtype=jnp.int32), lists.reshape(-1), rows)
    offered = jnp.dot(flat, picker, preferred_element_type=jnp.float32).astype(jnp.bfloat16)
    outgoing = [offered[:, offset * width : (offset + 1) * width] for offset in range(3)]
    pieces = []
    for offset in range(3):
        if offset == 1:
            pieces.append(outgoing[1])
        else:
            pieces.append(from_behind(outgoing[offset], "tile", 1 - offset))
    pool = jnp.concatenate(pieces, 1)
    placer = block_onehot(jnp.arange(3 * entries, dtype=jnp.int32), slots, rows)
    warped = jnp.dot(pool, placer, preferred_element_type=jnp.float32).astype(jnp.bfloat16)
    return warped.reshape(chan, rows, cols)


def on_device(frame_feats, send_list, recv_slot, w_unite, w_inner, w_outer, w_up):
    frames, chan, rows, cols = frame_feats.shape
    h = HALO
    origin = tile_origin(rows, cols)
    w1 = w_unite.transpose(0, 1, 3, 2).reshape(9, 2 * chan, chan)
    w2 = w_inner.transpose(0, 1, 3, 2).reshape(9, chan, chan)
    w3 = w_outer.transpose(0, 1, 3, 2).reshape(9, chan, chan)
    planes = w_up.shape[0]
    w_out = jnp.concatenate([w_up, jnp.eye(chan, dtype=w_up.dtype)], 0)

    def finish(x_ext, w_first):
        out = conv_chain(origin, to_flat(x_ext), w_first, w2, w3, w_out, rows)
        out = out.reshape(planes + chan, rows, PITCH)
        state, image = out[planes:, :, :cols], out[:planes]
        return state, image

    state, first = finish(with_halo(frame_feats[0], h), w1[:, chan:, :])

    def advance(state, inputs):
        feats, lists, slots = inputs
        warped = move_blocks(state, lists, slots)
        joined_ext = with_halo(jnp.concatenate([warped, feats], 0), h)
        return finish(joined_ext, w1)

    _, rest = lax.scan(
        advance, state, (frame_feats[1:], send_list[1:, 0, 0], recv_slot[1:, 0, 0])
    )
    return jnp.concatenate([first[None], rest], 0)[..., :cols]


def solution(mesh):
    placed = (
        P(None, None, "tile", "tm"),
        P(None, "tm", "tile", None, None),
        P(None, "tm", "tile", None),
        P(),
        P(),
        P(),
        P(),
    )
    return jax.shard_map(
        on_device,
        mesh=mesh,
        in_specs=placed,
        out_specs=P(None, None, "tile", "tm"),
        check_vma=False,
    )
```

```python
import jax
import jax.numpy as jnp
from jax import lax
from jax.sharding import PartitionSpec as P
from jax.experimental import pallas as pl
from jax.experimental.pallas import tpu as pltpu

HALO = 3


def shifted(value, moves):
    d_tm, d_tile = moves
    n_tm, n_tile = lax.axis_size("tm"), lax.axis_size("tile")
    pairs = []
    for a in range(n_tm):
        for b in range(n_tile):
            a2, b2 = a + d_tm, b + d_tile
            if 0 <= a2 < n_tm and 0 <= b2 < n_tile:
                pairs.append((a * n_tile + b, a2 * n_tile + b2))
    return lax.ppermute(value, ("tm", "tile"), pairs)


def with_halo(value, width):
    cols = value.shape[-1]
    west = shifted(value[..., :, cols - width :], (1, 0))
    east = shifted(value[..., :, :width], (-1, 0))
    middle = jnp.concatenate([west, value, east], -1)
    rows = middle.shape[-2]
    above = shifted(middle[..., rows - width :, :], (0, 1))
    below = shifted(middle[..., :width, :], (0, -1))
    return jnp.concatenate([above, middle, below], -2)


PITCH = 272


def flat_conv(src_ref, w_ref, out_rows):
    size = out_rows * PITCH
    total = None
    for b in range(3):
        part = None
        for a in range(3):
            term = jnp.dot(src_ref[a * PITCH : a * PITCH + size, :], w_ref[a * 3 + b],
                           preferred_element_type=jnp.float32)
            part = term if part is None else part + term
        if b:
            part = pltpu.roll(part, size - b, 0)
        total = part if total is None else total + part
    return total


def crop_mask(org_ref, out_rows, margin, chan):
    y = lax.broadcasted_iota(jnp.int32, (out_rows, PITCH, chan), 0)
    x = lax.broadcasted_iota(jnp.int32, (out_rows, PITCH, chan), 1)
    r = org_ref[0] - margin + y
    c = org_ref[1] - margin + x
    width = org_ref[4]
    ok = (r >= 0) & (r < org_ref[2]) & (c >= 0) & (c < org_ref[3]) & (x < width + 2 * margin)
    return ok.astype(jnp.float32)


def masked(acc, mask):
    rows = mask.shape[0]
    return (acc.reshape(rows, PITCH, acc.shape[-1]) * mask).reshape(acc.shape)


def chain_kernel(org_ref, x_ref, w1_ref, w2_ref, w3_ref, wup_ref, img_ref, u_ref, i_ref):
    rows = img_ref.shape[1] // PITCH
    chan = u_ref.shape[1]
    m1 = crop_mask(org_ref, rows + 4, 2, chan)
    u_ref[...] = masked(flat_conv(x_ref, w1_ref, rows + 4), m1).astype(jnp.bfloat16)
    m2 = crop_mask(org_ref, rows + 2, 1, chan)
    inner = jnp.maximum(flat_conv(u_ref, w2_ref, rows + 2), 0.0)
    i_ref[...] = masked(inner, m2).astype(jnp.bfloat16)
    size = rows * PITCH
    res = pltpu.roll(u_ref[2 * PITCH : 2 * PITCH + size, :].astype(jnp.float32), size - 2, 0)
    st = (res + flat_conv(i_ref, w3_ref, rows)).astype(jnp.bfloat16)
    img = lax.dot_general(wup_ref[...], st, (((1,), (1,)), ((), ())), preferred_element_type=jnp.float32)
    img_ref[...] = img.astype(jnp.bfloat16)


def conv_chain(origin, x_flat, w1, w2, w3, wup, rows):
    chan, planes = w2.shape[1], wup.shape[0]
    vmem = pl.BlockSpec(memory_space=pltpu.VMEM)
    return pl.pallas_call(
        chain_kernel,
        out_shape=jax.ShapeDtypeStruct((planes, rows * PITCH), jnp.bfloat16),
        in_specs=[pl.BlockSpec(memory_space=pltpu.SMEM)] + [vmem] * 5,
        out_specs=vmem,
        scratch_shapes=[
            pltpu.VMEM(((rows + 4) * PITCH, chan), jnp.bfloat16),
            pltpu.VMEM(((rows + 2) * PITCH, chan), jnp.bfloat16),
        ],
    )(origin, x_flat, w1, w2, w3, wup)


def to_flat(x_ext):
    k, h, w = x_ext.shape
    hwc = jnp.pad(x_ext.transpose(1, 2, 0), ((0, 0), (0, PITCH - w), (0, 0)))
    return hwc.reshape(h * PITCH, k)


def tile_origin(rows, cols):
    n_tm, n_tile = lax.axis_size("tm"), lax.axis_size("tile")
    band, strip = lax.axis_index("tile"), lax.axis_index("tm")
    return jnp.stack([band * rows, strip * cols, jnp.int32(rows * n_tile), jnp.int32(cols * n_tm), jnp.int32(cols)]).astype(jnp.int32)


def from_behind(value, axis, by):
    size = lax.axis_size(axis)
    pairs = [(i, i + by) for i in range(size) if 0 <= i + by < size]
    return lax.ppermute(value, axis, pairs)


def block_onehot(rows_of, cols_of, blk):
    row_ids = jnp.broadcast_to(rows_of[:, None], (rows_of.shape[0], blk)).reshape(-1)
    col_ids = jnp.broadcast_to(cols_of[:, None], (cols_of.shape[0], blk)).reshape(-1)
    i = jnp.arange(row_ids.shape[0], dtype=jnp.int32)
    j = jnp.arange(col_ids.shape[0], dtype=jnp.int32)
    same = (row_ids[:, None] == col_ids[None, :]) & ((i % blk)[:, None] == (j % blk)[None, :])
    return same.astype(jnp.bfloat16)


def move_blocks(state, lists, slots):
    chan, rows, cols = state.shape
    entries = lists.shape[1]
    width = entries * rows
    blocks = cols // rows
    flat = state.reshape(chan * rows, cols)
    picker = block_onehot(jnp.arange(blocks, dtype=jnp.int32), lists.reshape(-1), rows)
    offered = jnp.dot(flat, picker, preferred_element_type=jnp.float32).astype(jnp.bfloat16)
    outgoing = [offered[:, offset * width : (offset + 1) * width] for offset in range(3)]
    pieces = []
    for offset in range(3):
        if offset == 1:
            pieces.append(outgoing[1])
        else:
            pieces.append(from_behind(outgoing[offset], "tile", 1 - offset))
    pool = jnp.concatenate(pieces, 1)
    placer = block_onehot(jnp.arange(3 * entries, dtype=jnp.int32), slots, rows)
    warped = jnp.dot(pool, placer, preferred_element_type=jnp.float32).astype(jnp.bfloat16)
    return warped.reshape(chan, rows, cols)


def on_device(frame_feats, send_list, recv_slot, w_unite, w_inner, w_outer, w_up):
    frames, chan, rows, cols = frame_feats.shape
    h = HALO
    origin = tile_origin(rows, cols)
    w1 = w_unite.transpose(0, 1, 3, 2).reshape(9, 2 * chan, chan)
    w2 = w_inner.transpose(0, 1, 3, 2).reshape(9, chan, chan)
    w3 = w_outer.transpose(0, 1, 3, 2).reshape(9, chan, chan)
    planes = w_up.shape[0]
    w_out = jnp.concatenate([w_up, jnp.eye(chan, dtype=w_up.dtype)], 0)

    def finish(x_ext, w_first):
        out = conv_chain(origin, to_flat(x_ext), w_first, w2, w3, w_out, rows)
        out = out.reshape(planes + chan, rows, PITCH)
        state, image = out[planes:, :, :cols], out[:planes]
        return state, image

    state, first = finish(with_halo(frame_feats[0], h), w1[:, chan:, :])

    def advance(state, inputs):
        feats, lists, slots = inputs
        warped = move_blocks(state, lists, slots)
        joined_ext = with_halo(jnp.concatenate([warped, feats], 0), h)
        return finish(joined_ext, w1)

    _, rest = lax.scan(
        advance, state, (frame_feats[1:], send_list[1:, 0, 0], recv_slot[1:, 0, 0])
    )
    return jnp.concatenate([first[None], rest], 0)[..., :cols]


def solution(mesh):
    placed = (
        P(None, None, "tile", "tm"),
        P(None, "tm", "tile", None, None),
        P(None, "tm", "tile", None),
        P(),
        P(),
        P(),
        P(),
    )
    return jax.shard_map(
        on_device,
        mesh=mesh,
        in_specs=placed,
        out_specs=P(None, None, "tile", "tm"),
        check_vma=False,
    )
```
